256 devices in a mesh: req: 32 (over z, x), tp: 8 (over y, core).
Axes of the slice: x: 4, y: 4, z: 8, core: 2. Of those that a mesh axis runs over, the one named last changes fastest.
Arguments:
- hidden: bfloat16 [8192, 2048], P('req'), may hold values from -6 to 6
- kv_cache: bfloat16 [2, 1024, 128, 2048], P(None, 'req', None, 'tp'), may hold values from -64 to 64
- page_table: int32 [128, 8], P('req'), may hold values from 0 to 31, as said below
- cache_lens: int32 [128], P('req'), may hold values from 1 to 1024
- parents: int32 [128, 64], P('req'), may hold values from 0 to 62, as said below
- accepted: int32 [128, 8], P('req'), may hold values from 0 to 14, as said below
- attn_gain: float32 [2048], replicated, may hold values from 0.1 to 1.9
- w_qkv: bfloat16 [2048, 3, 2048], P(None, None, 'tp'), may hold values from -0.125 to 0.125
- qk_gain: float32 [2, 2048], P(None, 'tp'), may hold values from 0.5 to 8
- w_out: bfloat16 [2048, 2048], P('tp'), may hold values from -0.5 to 0.5
- moe_gain: float32 [2048], replicated, may hold values from 0.1 to 1.9
- routes: int32 [8192, 8], P('req'), may hold values from 0 to 63, all different within a row; in each aligned block of 256 rows (0 to 255, 256 to 511, ...) at most 40 rows name the same one
- route_weights: float32 [8192, 8], P('req'), may hold values from 0.1 to 1
- w_gate_up: bfloat16 [32, 2048, 2, 2048], P('req', None, None, 'tp'), may hold values from -0.125 to 0.125
- w_down: bfloat16 [32, 2048, 2048], P('req', 'tp'), may hold values from -0.1875 to 0.1875
Outputs:
- output: bfloat16 [8192, 2048], P('req', 'tp')
- accepted_kv: bfloat16 [2, 1024, 2048], P(None, 'req', 'tp')
The draws below stay inside these ranges and needn't reach their ends.
Inputs may be any that keep to these rules, and one draw needn't show every extreme that they name: `page_table`: values lie in the block of 32 pages of the request's group of 4 requests; within a group every page is used once. parents[r, 0] = 0 and parents[r, j] < j for j >= 1. accepted[r] are the first 8 slots, from the root down, of a path in request r's tree. `routes`: in each aligned block of 256 rows (the tokens of one index of req), no expert is named by more than 40 rows.
All inputs are finite; a program needn't handle non-finite values.
Results may differ from the reference program's by a relative error of at most 0.012.
The reference program's roundings to bfloat16 on the way count: a program that leaves them out, or rounds other values in their place, can miss the bound.
Values may be sent and summed in bfloat16 or wider, within the bound.
No kernel may reach another device: no remote copies, remote signals or barrier semaphores. Data moves between devices by JAX's collectives and lax.ppermute only.
A program may use at most 128 MiB of HBM per device.

```python
import math
import jax
import jax.numpy as jnp
import numpy as np
from jax import lax

D = 2048
HEADS = 16
HD = 128
FFE = 1024
EXPERTS = 64
TOPK = 8
PAGE = 128
DRAFT = 64
ACC = 8
PAGES_REQ = 8
REQ_DEV = 4
TOK_DEV = 256
REQUESTS = 128
TOKENS = 8192
EPR = 2
HB = 256
CAP = 40
N_REQ = 32


def draw_qk_gain(key, part):
    subkey = jax.random.fold_in(key, 31)
    return jax.random.uniform(subkey, (2, D), jnp.float32, 0.6, 1.6)


def draw_kv_cache(key, part):
    subkey = jax.random.fold_in(key, 41)
    base_draw = jnp.clip(jax.random.normal(subkey, (2, REQUESTS * PAGES_REQ, PAGE, D), jnp.float32), -6.0, 6.0)
    return base_draw.astype(jnp.bfloat16)


def draw_cache_lens(key, part):
    subkey = jax.random.fold_in(key, 51)
    longest = PAGES_REQ * PAGE
    levels = jax.random.randint(jax.random.fold_in(subkey, 1), (REQUESTS // REQ_DEV,), 1, 5)
    spread = jnp.repeat(levels, REQ_DEV)
    base_draw = jax.random.randint(jax.random.fold_in(subkey, 2), (REQUESTS,), 0, longest)
    lengths = 1 + base_draw * spread // 4
    return lengths.at[0].set(longest).astype(jnp.int32)


def draw_page_table(key, part):
    subkey = jax.random.fold_in(key, 61)
    group_keys = jax.random.split(subkey, REQUESTS // REQ_DEV)

    def shuffle(group_key):
        return jax.random.permutation(group_key, REQ_DEV * PAGES_REQ)
    orders = jax.vmap(shuffle)(group_keys)
    return orders.reshape(REQUESTS, PAGES_REQ).astype(jnp.int32)


def tree_draw(key):
    subkey = jax.random.fold_in(key, 71)
    steps_back = jax.random.randint(jax.random.fold_in(subkey, 1), (REQUESTS, DRAFT), 0, 2)
    head_slots = jnp.arange(1, 2 * ACC, dtype=jnp.int32)
    steps_back = steps_back.at[0, 1:2 * ACC].set(jnp.where(head_slots <= 2 * ACC - 2, 1, 0).astype(jnp.int32))
    steps_back = steps_back.at[0, DRAFT - 1].set(0)
    slot_ids = jnp.arange(DRAFT, dtype=jnp.int32)[None, :]
    parent_rows = jnp.where(slot_ids == 0, 0, jnp.maximum(slot_ids - 1 - steps_back, 0)).astype(jnp.int32)
    leaf_back = jax.random.randint(jax.random.fold_in(subkey, 2), (REQUESTS,), 0, 3)
    leaf_slots = (DRAFT - 1 - leaf_back).astype(jnp.int32)

    def path_of(parent_row, leaf_slot):

        def deepen(slot_index, depths):
            return depths.at[slot_index].set(depths[parent_row[slot_index]] + 1)
        depths = lax.fori_loop(1, DRAFT, deepen, jnp.zeros((DRAFT,), jnp.int32))

        def climb(step_index, carry_state):
            current, chosen = carry_state
            level_here = depths[current]
            updated = chosen.at[jnp.minimum(level_here, ACC - 1)].set(current)
            chosen = jnp.where(level_here < ACC, updated, chosen)
            return (parent_row[current], chosen)
        finished = lax.fori_loop(0, DRAFT, climb, (leaf_slot, jnp.zeros((ACC,), jnp.int32)))
        return finished[1]
    accepted_rows = jax.vmap(path_of)(parent_rows, leaf_slots)
    return (parent_rows, accepted_rows.astype(jnp.int32))


def draw_parents(key, part):
    return tree_draw(key)[0]


def draw_accepted(key, part):
    return tree_draw(key)[1]


def block_levels(key, extent, shards, low, top_value):
    loudness, own = 1.0, jax.random.fold_in(key, 6)
    for position, blocks in shards:
        steps = jnp.exp(jax.random.uniform(jax.random.fold_in(own, position), (blocks,), jnp.float32, low / len(shards), top_value / len(shards)))
        loudness = loudness * jnp.repeat(steps, extent[position] // blocks).reshape([-1 if axis == position else 1 for axis in range(len(extent))])
    return loudness


def routed_block(rng, own, number, rows, number_of, top, reach, slope):
    sequence = jax.random.permutation(rng, number_of)
    heavy_load, usual = load_shares(number_of, rows * top, reach, slope, True), load_shares(number_of, rows * top, reach, slope, False)
    places = jnp.arange(number_of)

    def named(sizes, offset_by):
        used = int((sizes > 0).sum())
        fixed = max(1, used // 4)
        shifted = fixed + (places - fixed + offset_by * (used - fixed)) % max(1, number_of - fixed)
        return jnp.zeros((number_of,), jnp.int32).at[sequence[jnp.where(places < fixed, places, shifted)]].set(jnp.asarray(sizes, jnp.int32))

    sizes = jnp.where(number % 4 == 0, named(heavy_load, number // 4), named(usual, number - number // 4 - 1))
    mixed = jax.random.permutation(jax.random.fold_in(own, 3), number_of)
    source_of, taker = mixed[0:number_of // 2 * 2:2], mixed[1:number_of // 2 * 2:2]
    room = jnp.minimum(sizes[source_of] - 1, reach - sizes[taker]) // 2
    room = jnp.where((source_of == sequence[0]) | (taker == sequence[0]) | (sizes[taker] == 0), 0, jnp.maximum(room, 0))
    shifted = jax.random.randint(jax.random.fold_in(own, 4), (number_of // 2,), 0, 1 << 20) % (room + 1)
    sizes = sizes.at[source_of].add(-shifted).at[taker].add(shifted)
    items = jnp.searchsorted(jnp.cumsum(sizes), jnp.arange(rows * top), side="right").astype(jnp.int32)
    table = items.reshape(top, rows).T
    table = table[jax.random.permutation(jax.random.fold_in(own, 1), rows)]
    offset_by = jax.random.randint(jax.random.fold_in(own, 2), (rows, 1), 0, top)
    return jnp.take_along_axis(table, (jnp.arange(top)[None, :] + offset_by) % top, axis=1)


def load_shares(amount, total, limit, slope, full):
    portions = [(1 << 20) // math.isqrt(grade ** slope) + 1 for grade in range(1, amount + 1)]
    largest = limit if full else min(limit, max(-(-total // amount), total * portions[0] // sum(portions)))
    least = 1 if total - largest >= amount - 1 else 0
    counts, surplus = [largest] + [least] * (amount - 1), total - largest - least * (amount - 1)
    while surplus > 0:
        free = [i for i in range(1, amount) if counts[i] < largest] or [i for i in range(1, amount) if counts[i] < limit]
        mass, remaining = sum([portions[i] for i in free]), surplus
        for i in free:
            addition = min(limit - counts[i], max(1, remaining * portions[i] // mass), surplus)
            counts[i] = counts[i] + addition
            surplus = surplus - addition
    return np.array(counts)


def centred(key, extent, deviation, most, pieces=(), kind=jnp.bfloat16):
    drawn = deviation * jax.random.normal(key, extent, jnp.float32)
    if pieces:
        drawn = drawn * block_levels(key, extent, pieces, -0.22, 0.18)
    return jnp.clip(drawn, -most, most).astype(kind)


def setup_inputs(seed: int = 0) -> dict:
    key_list = jax.random.split(jax.random.key(seed), 16)
    hidden = centred(key_list[0], (TOKENS, D), 1.0, 6.0, ((0, 32),))
    kv_cache = draw_kv_cache(jax.random.fold_in(key_list[15], 71), 0)
    page_table = draw_page_table(jax.random.fold_in(key_list[15], 71), 0)
    cache_lens = draw_cache_lens(jax.random.fold_in(key_list[15], 71), 0)
    parents = draw_parents(jax.random.fold_in(key_list[15], 71), 0)
    accepted = draw_accepted(jax.random.fold_in(key_list[15], 71), 0)
    attn_gain = jnp.clip(1.0 + 0.18 * jax.random.normal(key_list[6], (D,), jnp.float32), 0.1, 1.9)
    w_qkv = centred(key_list[7], (D, 3, D), D ** -0.5, 0.125, ((2, 8),))
    qk_gain = draw_qk_gain(jax.random.fold_in(key_list[15], 71), 0)
    w_out = centred(key_list[9], (D, D), (D // 16) ** -0.5, 0.5, ((0, 8),))
    moe_gain = jnp.clip(1.0 + 0.18 * jax.random.normal(key_list[10], (D,), jnp.float32), 0.1, 1.9)
    routes_keys = jax.random.split(jax.random.fold_in(key_list[11], 1), TOKENS // TOK_DEV)
    routes_turns = jax.random.permutation(jax.random.fold_in(key_list[11], 3), TOKENS // TOK_DEV)
    routes = jax.vmap(lambda own, number: routed_block(jax.random.fold_in(key_list[11], 2), own, number, TOK_DEV, EXPERTS, TOPK, CAP, 1))(routes_keys, routes_turns).reshape((TOKENS, TOPK))
    route_weights = jnp.clip(jnp.exp(math.log(1.0) - 2.3025851 * jax.random.uniform(key_list[12], (TOKENS, TOPK), jnp.float32) ** block_levels(key_list[12], (TOKENS, TOPK), ((0, 32),), -0.2, 0.2)), 0.1, 1.0)
    w_gate_up = centred(key_list[13], (EXPERTS // EPR, D, 2, EPR * FFE), D ** -0.5, 0.125, ((0, 32), (3, 8)))
    w_down = centred(key_list[14], (EXPERTS // EPR, EPR * FFE, D), FFE ** -0.5, 0.1875, ((0, 32), (1, 8)))
    return {"hidden": hidden, "kv_cache": kv_cache, "page_table": page_table, "cache_lens": cache_lens, "parents": parents, "accepted": accepted, "attn_gain": attn_gain, "w_qkv": w_qkv, "qk_gain": qk_gain, "w_out": w_out, "moe_gain": moe_gain, "routes": routes, "route_weights": route_weights, "w_gate_up": w_gate_up, "w_down": w_down}


norm_eps = 1e-05
rope_base = 10000.0
masked_score = -1e+30

def rms_scale(values, gain):
    return values * lax.rsqrt(lax.optimization_barrier(jnp.mean(values * values, axis=-1, keepdims=True)) + norm_eps) * gain

def tree_masks(parents):
    slot_count = parents.shape[-1]
    slot_ids = jnp.arange(slot_count, dtype=jnp.int32)
    parent_hot = (parents[..., :, None] == slot_ids).astype(jnp.float32)
    ancestry = jnp.minimum(jnp.eye(slot_count, dtype=jnp.float32) + parent_hot, 1.0)
    for squaring in range(slot_count.bit_length()):
        ancestry = jnp.minimum(jnp.einsum('rij,rjk->rik', ancestry, ancestry, precision=lax.Precision.HIGHEST), 1.0)
    depths = lax.optimization_barrier(jnp.sum(ancestry, axis=-1)).astype(jnp.int32) - 1
    return (ancestry, depths)

def rotate(values, positions):
    head_dim = values.shape[-1]
    half_dim = head_dim // 2
    frequency = rope_base ** (-jnp.arange(half_dim, dtype=jnp.float32) * 2.0 / head_dim)
    angles = positions.astype(jnp.float32)[:, None] * frequency[None, :]
    cosine = jnp.cos(angles)[:, None, :]
    sine_part = jnp.sin(angles)[:, None, :]
    first_half = values[..., :half_dim]
    second = values[..., half_dim:]
    return jnp.concatenate([first_half * cosine - second * sine_part, second * cosine + first_half * sine_part], axis=-1)

def reference(hidden, kv_cache, page_table, cache_lens, parents, accepted, attn_gain, w_qkv, qk_gain, w_out, moe_gain, routes, route_weights, w_gate_up, w_down):
    ancestry, depths = tree_masks(parents)
    positions = (cache_lens[:, None] + depths).reshape(-1)
    normed_in = rms_scale(hidden.astype(jnp.float32), attn_gain).astype(jnp.bfloat16)
    projected = jnp.dot(normed_in, w_qkv.reshape(D, 3 * D), preferred_element_type=jnp.float32).reshape(TOKENS, 3, D)
    query_normed = rms_scale(projected[:, 0], qk_gain[0])
    key_normed = rms_scale(projected[:, 1], qk_gain[1])
    values_new = projected[:, 2].astype(jnp.bfloat16)
    query_rot = rotate(query_normed.reshape(TOKENS, HEADS, HD), positions).astype(jnp.bfloat16)
    keys_new = rotate(key_normed.reshape(TOKENS, HEADS, HD), positions).astype(jnp.bfloat16)
    context = PAGES_REQ * PAGE
    score_scale = HD ** (-0.5)

    def one_request(request):
        page_ids = request // REQ_DEV * (REQ_DEV * PAGES_REQ) + page_table[request]
        page_rows = kv_cache[:, page_ids].reshape(2, context, HEADS, HD).astype(jnp.float32)
        first_row = (request * DRAFT).astype(jnp.int32)
        queries = lax.dynamic_slice_in_dim(query_rot, first_row, DRAFT, 0).astype(jnp.float32)
        own_keys = lax.dynamic_slice_in_dim(keys_new, first_row, DRAFT, 0).astype(jnp.float32)
        own_values = lax.dynamic_slice_in_dim(values_new, first_row, DRAFT, 0).reshape(DRAFT, HEADS, HD).astype(jnp.float32)
        cache_scores = jnp.einsum('jhd,chd->hjc', queries, page_rows[0]) * score_scale
        live_keys = jnp.arange(context, dtype=jnp.int32) < cache_lens[request]
        cache_scores = jnp.where(live_keys[None, None, :], cache_scores, masked_score)
        draft_scores = jnp.einsum('jhd,ihd->hji', queries, own_keys) * score_scale
        draft_scores = jnp.where(ancestry[request][None, :, :] > 0.5, draft_scores, masked_score)
        scores = jnp.concatenate([cache_scores, draft_scores], axis=-1)
        row_max = lax.optimization_barrier(jnp.max(scores, axis=-1, keepdims=True))
        weights = jnp.exp(scores - row_max)
        probabilities = (weights / lax.optimization_barrier(jnp.sum(weights, axis=-1, keepdims=True))).astype(jnp.bfloat16).astype(jnp.float32)
        mixed = jnp.einsum('hjc,chd->jhd', probabilities[..., :context], page_rows[1])
        mixed = mixed + jnp.einsum('hji,ihd->jhd', probabilities[..., context:], own_values)
        return mixed.astype(jnp.bfloat16).reshape(DRAFT, D)
    attn_heads = lax.map(one_request, jnp.arange(REQUESTS, dtype=jnp.int32)).reshape(TOKENS, D)
    residual = hidden.astype(jnp.float32) + jnp.dot(attn_heads, w_out, preferred_element_type=jnp.float32)
    normed_moe = rms_scale(residual, moe_gain).astype(jnp.bfloat16)
    grouped = routes.reshape(N_REQ, TOK_DEV * TOPK)
    one_hot = (grouped[..., None] == jnp.arange(EXPERTS, dtype=jnp.int32)).astype(jnp.int32)
    slot_of = lax.optimization_barrier(jnp.sum((jnp.cumsum(one_hot, axis=1) - one_hot) * one_hot, axis=-1))
    columns = jnp.arange(N_REQ, dtype=jnp.int32)[:, None] * CAP + slot_of
    token_ids = (jnp.arange(N_REQ * TOK_DEV * TOPK, dtype=jnp.int32) // TOPK).reshape(N_REQ, TOK_DEV * TOPK)
    row_table = jnp.zeros((EXPERTS, N_REQ * CAP), jnp.int32).at[grouped, columns].set(token_ids)
    block_count = FFE // HB

    def one_expert(expert):
        group_id = (expert // EPR).astype(jnp.int32)
        first_unit = (expert % EPR * FFE).astype(jnp.int32)
        gate_up_w = lax.dynamic_slice_in_dim(w_gate_up[group_id], first_unit, FFE, 2)
        down_w = lax.dynamic_slice_in_dim(w_down[group_id], first_unit, FFE, 0)
        gathered = normed_moe[row_table[expert]]
        gate_up = jnp.dot(gathered, gate_up_w.reshape(D, 2 * FFE), preferred_element_type=jnp.float32).reshape(-1, 2, FFE)
        activated = (jax.nn.silu(gate_up[:, 0]) * gate_up[:, 1]).astype(jnp.bfloat16)
        block_parts = jnp.einsum('rnf,nfd->rnd', activated.reshape(-1, block_count, HB).astype(jnp.float32), down_w.reshape(block_count, HB, D).astype(jnp.float32))
        rounded = lax.optimization_barrier(block_parts.astype(jnp.bfloat16))
        return lax.optimization_barrier(jnp.sum(rounded.astype(jnp.float32), axis=1)).astype(jnp.bfloat16)
    expert_rows = lax.map(one_expert, jnp.arange(EXPERTS, dtype=jnp.int32))
    flat_experts = grouped.reshape(TOKENS, TOPK)
    flat_columns = columns.reshape(TOKENS, TOPK)
    mixture = jnp.zeros((TOKENS, D), jnp.float32)
    for route_rank in range(TOPK):
        chosen = expert_rows[flat_experts[:, route_rank], flat_columns[:, route_rank]].astype(jnp.float32)
        mixture = mixture + route_weights[:, route_rank:route_rank + 1] * chosen
    output = (residual + mixture).astype(jnp.bfloat16)
    picked_rows = (jnp.arange(REQUESTS, dtype=jnp.int32)[:, None] * DRAFT + accepted).reshape(-1)
    accepted_kv = jnp.stack([keys_new.reshape(TOKENS, D)[picked_rows], values_new[picked_rows]])
    return (output, accepted_kv)
```

```python
import jax
import jax.numpy as jnp
from jax import lax
from jax.sharding import Mesh, PartitionSpec as P

HD = 128
FFE = 1024
EXPERTS = 64
CAP = 40
TP = ("th", "tl", "tc")


norm_eps = 1e-05
rope_base = 10000.0
masked_score = -1e30


def rms_scale(values, gain):
    return values * lax.rsqrt(jnp.mean(values * values, axis=-1, keepdims=True) + norm_eps) * gain


def tree_masks(parents):
    slot_count = parents.shape[-1]
    slot_ids = jnp.arange(slot_count, dtype=jnp.int32)
    parent_hot = (parents[..., :, None] == slot_ids).astype(jnp.float32)
    ancestry = jnp.minimum(jnp.eye(slot_count, dtype=jnp.float32) + parent_hot, 1.0)
    for squaring in range(slot_count.bit_length()):
        ancestry = jnp.minimum(
            jnp.einsum("rij,rjk->rik", ancestry, ancestry, precision=lax.Precision.HIGHEST), 1.0
        )
    depths = jnp.sum(ancestry, axis=-1).astype(jnp.int32) - 1
    return (ancestry, depths)


def rotate(values, positions):
    head_dim = values.shape[-1]
    half_dim = head_dim // 2
    frequency = rope_base ** (-jnp.arange(half_dim, dtype=jnp.float32) * 2.0 / head_dim)
    angles = positions.astype(jnp.float32)[:, None] * frequency[None, :]
    cosine = jnp.cos(angles)[:, None, :]
    sine_part = jnp.sin(angles)[:, None, :]
    first_half = values[..., :half_dim]
    second = values[..., half_dim:]
    return jnp.concatenate(
        [first_half * cosine - second * sine_part, second * cosine + first_half * sine_part],
        axis=-1,
    )


def local(
    hidden,
    kv_cache,
    page_table,
    cache_lens,
    parents,
    accepted,
    attn_gain,
    w_qkv,
    qk_gain,
    w_out,
    moe_gain,
    routes,
    route_weights,
    w_gate_up,
    w_down,
):
    tok_rows, model_width = hidden.shape
    th = lax.axis_index("th")
    tl = lax.axis_index("tl")
    tc = lax.axis_index("tc")
    tp_count = lax.axis_size(TP)
    req_count = lax.axis_size("req")
    slice_width = model_width // tp_count
    slice_start = ((th * lax.axis_size("tl") + tl) * lax.axis_size("tc") + tc) * slice_width
    req_local, draft_len = parents.shape
    feat_dev = w_qkv.shape[2]
    local_heads = feat_dev // HD
    ancestry, depths = tree_masks(parents)
    positions = (cache_lens[:, None] + depths).reshape(-1)
    normed_in = rms_scale(hidden.astype(jnp.float32), attn_gain).astype(jnp.bfloat16)
    projected = jnp.dot(
        normed_in, w_qkv.reshape(model_width, 3 * feat_dev), preferred_element_type=jnp.float32
    ).reshape(tok_rows, 3, feat_dev)
    query_raw = projected[:, 0]
    key_raw = projected[:, 1]
    values_new = projected[:, 2].astype(jnp.bfloat16)
    query_total, key_total = lax.psum(
        (jnp.sum(query_raw * query_raw, axis=-1), jnp.sum(key_raw * key_raw, axis=-1)), TP
    )
    query_normed = query_raw * lax.rsqrt(query_total[:, None] / model_width + norm_eps) * qk_gain[0]
    key_normed = key_raw * lax.rsqrt(key_total[:, None] / model_width + norm_eps) * qk_gain[1]
    query_rot = rotate(query_normed.reshape(tok_rows, local_heads, HD), positions).astype(
        jnp.bfloat16
    )
    keys_new = rotate(key_normed.reshape(tok_rows, local_heads, HD), positions).astype(jnp.bfloat16)
    page_rows = kv_cache[:, page_table.reshape(-1)]
    context = page_table.shape[1] * kv_cache.shape[2]
    cache_keys = page_rows[0].reshape(req_local, context, local_heads, HD)
    cache_values = page_rows[1].reshape(req_local, context, local_heads, HD)
    query_blocks = query_rot.reshape(req_local, draft_len, local_heads, HD)
    key_blocks = keys_new.reshape(req_local, draft_len, local_heads, HD)
    value_blocks = values_new.reshape(req_local, draft_len, local_heads, HD)
    score_scale = HD ** (-0.5)
    cache_scores = (
        jnp.einsum("rjhd,rchd->rhjc", query_blocks, cache_keys, preferred_element_type=jnp.float32)
        * score_scale
    )
    live_keys = jnp.arange(context, dtype=jnp.int32)[None, :] < cache_lens[:, None]
    cache_scores = jnp.where(live_keys[:, None, None, :], cache_scores, masked_score)
    draft_scores = (
        jnp.einsum("rjhd,rihd->rhji", query_blocks, key_blocks, preferred_element_type=jnp.float32)
        * score_scale
    )
    draft_scores = jnp.where(ancestry[:, None, :, :] > 0.5, draft_scores, masked_score)
    scores = jnp.concatenate([cache_scores, draft_scores], axis=-1)
    row_max = jnp.max(scores, axis=-1, keepdims=True)
    weights = jnp.exp(scores - row_max)
    probabilities = (weights / jnp.sum(weights, axis=-1, keepdims=True)).astype(jnp.bfloat16)
    all_values = jnp.concatenate([cache_values, value_blocks], axis=1)
    attn_heads = (
        jnp.einsum("rhjc,rchd->rjhd", probabilities, all_values, preferred_element_type=jnp.float32)
        .astype(jnp.bfloat16)
        .reshape(tok_rows, feat_dev)
    )
    attn_term = jnp.dot(attn_heads, w_out, preferred_element_type=jnp.float32)
    residual = hidden.astype(jnp.float32) + lax.psum(attn_term, TP)
    normed_moe = rms_scale(residual, moe_gain).astype(jnp.bfloat16)
    residual_share = lax.dynamic_slice_in_dim(residual, slice_start, slice_width, 1)
    experts_here = EXPERTS // req_count
    tok_ids = jnp.arange(tok_rows, dtype=jnp.int32)
    route_hot = (routes[:, :, None] == jnp.arange(EXPERTS, dtype=jnp.int32)).astype(jnp.float32)
    per_token = jnp.sum(route_hot, axis=1)
    weight_of = jnp.sum(route_weights[:, :, None] * route_hot, axis=1)
    earlier = (tok_ids[:, None] > tok_ids[None, :]).astype(jnp.bfloat16)
    slot_of = jnp.dot(earlier, per_token.astype(jnp.bfloat16), preferred_element_type=jnp.float32)
    capacity = CAP
    cap_ids = jnp.arange(capacity, dtype=jnp.float32)
    picked_here = lax.dynamic_index_in_dim(
        per_token.reshape(tok_rows, req_count, experts_here), th, axis=2, keepdims=False
    ).T
    slot_here = lax.dynamic_index_in_dim(
        slot_of.reshape(tok_rows, req_count, experts_here), th, axis=2, keepdims=False
    ).T
    select = jnp.where(
        (picked_here[:, None, :] > 0.5) & (slot_here[:, None, :] == cap_ids[None, :, None]), 1.0, 0.0
    ).astype(jnp.bfloat16)
    half_width = model_width // 2
    normed_half = lax.dynamic_slice_in_dim(normed_moe, tc * half_width, half_width, 1)
    send_rows = jnp.einsum(
        "ict,tw->icw", select, normed_half, preferred_element_type=jnp.float32
    ).astype(jnp.bfloat16)
    received = lax.all_to_all(send_rows, "req", 0, 0, tiled=True)
    rows = lax.all_gather(received, "tc", axis=2, tiled=True)
    gate_up = jnp.einsum(
        "scw,wgu->scgu", rows, w_gate_up[0], preferred_element_type=jnp.float32
    )
    activated = (jax.nn.silu(gate_up[..., 0, :]) * gate_up[..., 1, :]).astype(jnp.bfloat16)
    units_dev = w_down.shape[1]
    down = w_down[0].reshape(units_dev, 2, 2, 2, slice_width)
    partial = jnp.einsum(
        "scu,uhlkd->shckld", activated, down, preferred_element_type=jnp.float32
    ).astype(jnp.bfloat16)
    partial = partial.reshape(req_count, 2, capacity, 4 * slice_width)
    partial = lax.psum_scatter(partial, "tc", scatter_dimension=3, tiled=True)
    partial = lax.psum_scatter(partial, "tl", scatter_dimension=3, tiled=True)
    back = partial.reshape(req_count * 2, capacity, slice_width)
    returned = lax.all_to_all(back, ("req", "th"), 0, 0, tiled=True)
    combine = weight_of[:, :, None] * (slot_of[:, :, None] == cap_ids[None, None, :])
    mixture = jnp.dot(
        combine.reshape(tok_rows, EXPERTS * capacity),
        returned.reshape(EXPERTS * capacity, slice_width).astype(jnp.float32),
        precision=lax.Precision.HIGHEST,
        preferred_element_type=jnp.float32,
    )
    output = (residual_share + mixture).astype(jnp.bfloat16)
    picked_rows = (jnp.arange(req_local, dtype=jnp.int32)[:, None] * draft_len + accepted).reshape(
        -1
    )
    accepted_kv = jnp.stack(
        [keys_new.reshape(tok_rows, feat_dev)[picked_rows], values_new[picked_rows]]
    )
    return (output, accepted_kv)


def solution(mesh):
    req_count = mesh.shape["req"]
    devices = mesh.devices.reshape(req_count, 2, 2, mesh.shape["tp"] // 4)
    split_mesh = Mesh(devices, ("req",) + TP)
    return jax.shard_map(
        local,
        mesh=split_mesh,
        in_specs=(
            P("req", None),
            P(None, "req", None, TP),
            P("req", None),
            P("req"),
            P("req", None),
            P("req", None),
            P(),
            P(None, None, TP),
            P(None, TP),
            P(TP, None),
            P(),
            P("req", None),
            P("req", None),
            P("req", None, None, TP),
            P("req", TP, None),
        ),
        out_specs=(P("req", TP), P(None, "req", TP)),
        check_vma=False,
    )
```

```python
import jax
import jax.numpy as jnp
from jax import lax
from jax.sharding import Mesh, PartitionSpec as P

HD = 128
FFE = 1024
EXPERTS = 64
CAP = 40
TP = ("th", "tl", "tc")


norm_eps = 1e-05
rope_base = 10000.0
masked_score = -1e30


def rms_scale(values, gain):
    return values * lax.rsqrt(jnp.mean(values * values, axis=-1, keepdims=True) + norm_eps) * gain


def tree_masks(parents):
    slot_count = parents.shape[-1]
    slot_ids = jnp.arange(slot_count, dtype=jnp.int32)
    parent_hot = (parents[..., :, None] == slot_ids).astype(jnp.float32)
    ancestry = jnp.minimum(jnp.eye(slot_count, dtype=jnp.float32) + parent_hot, 1.0)
    for squaring in range(slot_count.bit_length()):
        ancestry = jnp.minimum(
            jnp.einsum("rij,rjk->rik", ancestry, ancestry, precision=lax.Precision.HIGHEST), 1.0
        )
    depths = jnp.sum(ancestry, axis=-1).astype(jnp.int32) - 1
    return (ancestry, depths)


def rotate(values, positions):
    head_dim = values.shape[-1]
    half_dim = head_dim // 2
    frequency = rope_base ** (-jnp.arange(half_dim, dtype=jnp.float32) * 2.0 / head_dim)
    angles = positions.astype(jnp.float32)[:, None] * frequency[None, :]
    cosine = jnp.cos(angles)[:, None, :]
    sine_part = jnp.sin(angles)[:, None, :]
    first_half = values[..., :half_dim]
    second = values[..., half_dim:]
    return jnp.concatenate(
        [first_half * cosine - second * sine_part, second * cosine + first_half * sine_part],
        axis=-1,
    )


def local(
    hidden,
    kv_cache,
    page_table,
    cache_lens,
    parents,
    accepted,
    attn_gain,
    w_qkv,
    qk_gain,
    w_out,
    moe_gain,
    routes,
    route_weights,
    w_gate_up,
    w_down,
):
    tok_rows, model_width = hidden.shape
    th = lax.axis_index("th")
    tl = lax.axis_index("tl")
    tc = lax.axis_index("tc")
    tp_count = lax.axis_size(TP)
    req_count = lax.axis_size("req")
    slice_width = model_width // tp_count
    slice_start = ((th * lax.axis_size("tl") + tl) * lax.axis_size("tc") + tc) * slice_width
    req_local, draft_len = parents.shape
    feat_dev = w_qkv.shape[2]
    local_heads = feat_dev // HD
    ancestry, depths = tree_masks(parents)
    positions = (cache_lens[:, None] + depths).reshape(-1)
    normed_in = rms_scale(hidden.astype(jnp.float32), attn_gain).astype(jnp.bfloat16)
    projected = jnp.dot(
        normed_in, w_qkv.reshape(model_width, 3 * feat_dev), preferred_element_type=jnp.float32
    ).reshape(tok_rows, 3, feat_dev)
    query_raw = projected[:, 0]
    key_raw = projected[:, 1]
    values_new = projected[:, 2].astype(jnp.bfloat16)
    query_total, key_total = lax.psum(
        (jnp.sum(query_raw * query_raw, axis=-1), jnp.sum(key_raw * key_raw, axis=-1)), TP
    )
    query_normed = query_raw * lax.rsqrt(query_total[:, None] / model_width + norm_eps) * qk_gain[0]
    key_normed = key_raw * lax.rsqrt(key_total[:, None] / model_width + norm_eps) * qk_gain[1]
    query_rot = rotate(query_normed.reshape(tok_rows, local_heads, HD), positions).astype(
        jnp.bfloat16
    )
    keys_new = rotate(key_normed.reshape(tok_rows, local_heads, HD), positions).astype(jnp.bfloat16)
    page_rows = kv_cache[:, page_table.reshape(-1)]
    context = page_table.shape[1] * kv_cache.shape[2]
    cache_keys = page_rows[0].reshape(req_local, context, local_heads, HD)
    cache_values = page_rows[1].reshape(req_local, context, local_heads, HD)
    query_blocks = query_rot.reshape(req_local, draft_len, local_heads, HD)
    key_blocks = keys_new.reshape(req_local, draft_len, local_heads, HD)
    value_blocks = values_new.reshape(req_local, draft_len, local_heads, HD)
    score_scale = HD ** (-0.5)
    cache_scores = (
        jnp.einsum("rjhd,rchd->rhjc", query_blocks, cache_keys, preferred_element_type=jnp.float32)
        * score_scale
    )
    live_keys = jnp.arange(context, dtype=jnp.int32)[None, :] < cache_lens[:, None]
    cache_scores = jnp.where(live_keys[:, None, None, :], cache_scores, masked_score)
    draft_scores = (
        jnp.einsum("rjhd,rihd->rhji", query_blocks, key_blocks, preferred_element_type=jnp.float32)
        * score_scale
    )
    draft_scores = jnp.where(ancestry[:, None, :, :] > 0.5, draft_scores, masked_score)
    scores = jnp.concatenate([cache_scores, draft_scores], axis=-1)
    row_max = jnp.max(scores, axis=-1, keepdims=True)
    weights = jnp.exp(scores - row_max)
    probabilities = (weights / jnp.sum(weights, axis=-1, keepdims=True)).astype(jnp.bfloat16)
    all_values = jnp.concatenate([cache_values, value_blocks], axis=1)
    attn_heads = (
        jnp.einsum("rhjc,rchd->rjhd", probabilities, all_values, preferred_element_type=jnp.float32)
        .astype(jnp.bfloat16)
        .reshape(tok_rows, feat_dev)
    )
    attn_term = jnp.dot(attn_heads, w_out, preferred_element_type=jnp.float32)
    residual = hidden.astype(jnp.float32) + lax.psum(attn_term, TP)
    normed_moe = rms_scale(residual, moe_gain).astype(jnp.bfloat16)
    residual_share = lax.dynamic_slice_in_dim(residual, slice_start, slice_width, 1)
    experts_here = EXPERTS // req_count
    tok_ids = jnp.arange(tok_rows, dtype=jnp.int32)
    route_hot = (routes[:, :, None] == jnp.arange(EXPERTS, dtype=jnp.int32)).astype(jnp.float32)
    per_token = jnp.sum(route_hot, axis=1)
    weight_of = jnp.sum(route_weights[:, :, None] * route_hot, axis=1)
    earlier = (tok_ids[:, None] > tok_ids[None, :]).astype(jnp.bfloat16)
    slot_of = jnp.dot(earlier, per_token.astype(jnp.bfloat16), preferred_element_type=jnp.float32)
    capacity = CAP
    cap_ids = jnp.arange(capacity, dtype=jnp.float32)
    picked_here = lax.dynamic_index_in_dim(
        per_token.reshape(tok_rows, req_count, experts_here), th, axis=2, keepdims=False
    ).T
    slot_here = lax.dynamic_index_in_dim(
        slot_of.reshape(tok_rows, req_count, experts_here), th, axis=2, keepdims=False
    ).T
    select = jnp.where(
        (picked_here[:, None, :] > 0.5) & (slot_here[:, None, :] == cap_ids[None, :, None]), 1.0, 0.0
    ).astype(jnp.bfloat16)
    half_width = model_width // 2
    normed_half = lax.dynamic_slice_in_dim(normed_moe, tc * half_width, half_width, 1)
    send_rows = jnp.einsum(
        "ict,tw->icw", select, normed_half, preferred_element_type=jnp.float32
    ).astype(jnp.bfloat16)
    received = lax.all_to_all(send_rows, "req", 0, 0, tiled=True)
    partner_rows = lax.ppermute(received, "tc", [(0, 1), (1, 0)])
    own_weights = lax.dynamic_slice_in_dim(w_gate_up[0], tc * half_width, half_width, 0)
    partner_weights = lax.dynamic_slice_in_dim(w_gate_up[0], (1 - tc) * half_width, half_width, 0)
    gate_up = jnp.einsum(
        "scw,wgu->scgu", received, own_weights, preferred_element_type=jnp.float32
    ) + jnp.einsum(
        "scw,wgu->scgu", partner_rows, partner_weights, preferred_element_type=jnp.float32
    )
    activated = (jax.nn.silu(gate_up[..., 0, :]) * gate_up[..., 1, :]).astype(jnp.bfloat16)
    units_dev = w_down.shape[1]
    down = (
        w_down[0]
        .reshape(units_dev, 2, 2, 2, slice_width)
        .transpose(0, 3, 2, 1, 4)
        .reshape(units_dev, model_width)
    )
    partial = jnp.einsum(
        "scu,uw->scw", activated, down, preferred_element_type=jnp.float32
    ).astype(jnp.bfloat16)
    swap = [(0, 1), (1, 0)]
    half = model_width // 2
    kept = lax.dynamic_slice_in_dim(partial, tc * half, half, 2)
    given = lax.dynamic_slice_in_dim(partial, (1 - tc) * half, half, 2)
    pair_sum = kept.astype(jnp.float32) + lax.ppermute(given, "tc", swap).astype(jnp.float32)
    quarter = half // 2
    kept = lax.dynamic_slice_in_dim(pair_sum, tl * quarter, quarter, 2)
    given = lax.dynamic_slice_in_dim(pair_sum, (1 - tl) * quarter, quarter, 2).astype(jnp.bfloat16)
    quad_sum = (kept + lax.ppermute(given, "tl", swap).astype(jnp.float32)).astype(jnp.bfloat16)
    back = (
        quad_sum.reshape(req_count, capacity, 2, slice_width)
        .transpose(0, 2, 1, 3)
        .reshape(req_count * 2, capacity, slice_width)
    )
    returned = lax.all_to_all(back, ("req", "th"), 0, 0, tiled=True)
    combine = weight_of[:, :, None] * (slot_of[:, :, None] == cap_ids[None, None, :])
    mixture = jnp.dot(
        combine.reshape(tok_rows, EXPERTS * capacity),
        returned.reshape(EXPERTS * capacity, slice_width).astype(jnp.float32),
        precision=lax.Precision.HIGHEST,
        preferred_element_type=jnp.float32,
    )
    output = (residual_share + mixture).astype(jnp.bfloat16)
    picked_rows = (jnp.arange(req_local, dtype=jnp.int32)[:, None] * draft_len + accepted).reshape(
        -1
    )
    accepted_kv = jnp.stack(
        [keys_new.reshape(tok_rows, feat_dev)[picked_rows], values_new[picked_rows]]
    )
    return (output, accepted_kv)


def solution(mesh):
    req_count = mesh.shape["req"]
    devices = mesh.devices.reshape(req_count, 2, 2, mesh.shape["tp"] // 4)
    split_mesh = Mesh(devices, ("req",) + TP)
    return jax.shard_map(
        local,
        mesh=split_mesh,
        in_specs=(
            P("req", None),
            P(None, "req", None, TP),
            P("req", None),
            P("req"),
            P("req", None),
            P("req", None),
            P(),
            P(None, None, TP),
            P(None, TP),
            P(TP, None),
            P(),
            P("req", None),
            P("req", None),
            P("req", None, None, TP),
            P("req", TP, None),
        ),
        out_specs=(P("req", TP), P(None, "req", TP)),
        check_vma=False,
    )
```

```python
import jax
import jax.numpy as jnp
from jax import lax
from jax.sharding import Mesh, PartitionSpec as P

HD = 128
FFE = 1024
EXPERTS = 64
CAP = 40
TP = ("th", "tl", "tc")


norm_eps = 1e-05
rope_base = 10000.0
masked_score = -1e30


def rms_scale(values, gain):
    return values * lax.rsqrt(jnp.mean(values * values, axis=-1, keepdims=True) + norm_eps) * gain


def tree_masks(parents):
    slot_count = parents.shape[-1]
    slot_ids = jnp.arange(slot_count, dtype=jnp.int32)
    parent_hot = (parents[..., :, None] == slot_ids).astype(jnp.float32)
    ancestry = jnp.minimum(jnp.eye(slot_count, dtype=jnp.float32) + parent_hot, 1.0)
    for squaring in range(slot_count.bit_length()):
        ancestry = jnp.minimum(
            jnp.einsum("rij,rjk->rik", ancestry, ancestry, precision=lax.Precision.HIGHEST), 1.0
        )
    depths = jnp.sum(ancestry, axis=-1).astype(jnp.int32) - 1
    return (ancestry, depths)


def rotate(values, positions):
    head_dim = values.shape[-1]
    half_dim = head_dim // 2
    frequency = rope_base ** (-jnp.arange(half_dim, dtype=jnp.float32) * 2.0 / head_dim)
    angles = positions.astype(jnp.float32)[:, None] * frequency[None, :]
    cosine = jnp.cos(angles)[:, None, :]
    sine_part = jnp.sin(angles)[:, None, :]
    first_half = values[..., :half_dim]
    second = values[..., half_dim:]
    return jnp.concatenate(
        [first_half * cosine - second * sine_part, second * cosine + first_half * sine_part],
        axis=-1,
    )


def local(
    hidden,
    kv_cache,
    page_table,
    cache_lens,
    parents,
    accepted,
    attn_gain,
    w_qkv,
    qk_gain,
    w_out,
    moe_gain,
    routes,
    route_weights,
    w_gate_up,
    w_down,
):
    tok_rows, model_width = hidden.shape
    th = lax.axis_index("th")
    tl = lax.axis_index("tl")
    tc = lax.axis_index("tc")
    tp_count = lax.axis_size(TP)
    req_count = lax.axis_size("req")
    slice_width = model_width // tp_count
    slice_start = ((th * lax.axis_size("tl") + tl) * lax.axis_size("tc") + tc) * slice_width
    req_local, draft_len = parents.shape
    feat_dev = w_qkv.shape[2]
    local_heads = feat_dev // HD
    ancestry, depths = tree_masks(parents)
    positions = (cache_lens[:, None] + depths).reshape(-1)
    normed_in = rms_scale(hidden.astype(jnp.float32), attn_gain).astype(jnp.bfloat16)
    projected = jnp.dot(
        normed_in, w_qkv.reshape(model_width, 3 * feat_dev), preferred_element_type=jnp.float32
    ).reshape(tok_rows, 3, feat_dev)
    query_raw = projected[:, 0]
    key_raw = projected[:, 1]
    values_new = projected[:, 2].astype(jnp.bfloat16)
    query_total, key_total = lax.psum(
        (jnp.sum(query_raw * query_raw, axis=-1), jnp.sum(key_raw * key_raw, axis=-1)), TP
    )
    query_normed = query_raw * lax.rsqrt(query_total[:, None] / model_width + norm_eps) * qk_gain[0]
    key_normed = key_raw * lax.rsqrt(key_total[:, None] / model_width + norm_eps) * qk_gain[1]
    query_rot = rotate(query_normed.reshape(tok_rows, local_heads, HD), positions).astype(
        jnp.bfloat16
    )
    keys_new = rotate(key_normed.reshape(tok_rows, local_heads, HD), positions).astype(jnp.bfloat16)
    page_rows = kv_cache[:, page_table.reshape(-1)]
    context = page_table.shape[1] * kv_cache.shape[2]
    cache_keys = page_rows[0].reshape(req_local, context, local_heads, HD)
    cache_values = page_rows[1].reshape(req_local, context, local_heads, HD)
    query_blocks = query_rot.reshape(req_local, draft_len, local_heads, HD)
    key_blocks = keys_new.reshape(req_local, draft_len, local_heads, HD)
    value_blocks = values_new.reshape(req_local, draft_len, local_heads, HD)
    score_scale = HD ** (-0.5)
    cache_scores = (
        jnp.einsum("rjhd,rchd->rhjc", query_blocks, cache_keys, preferred_element_type=jnp.float32)
        * score_scale
    )
    live_keys = jnp.arange(context, dtype=jnp.int32)[None, :] < cache_lens[:, None]
    cache_scores = jnp.where(live_keys[:, None, None, :], cache_scores, masked_score)
    draft_scores = (
        jnp.einsum("rjhd,rihd->rhji", query_blocks, key_blocks, preferred_element_type=jnp.float32)
        * score_scale
    )
    draft_scores = jnp.where(ancestry[:, None, :, :] > 0.5, draft_scores, masked_score)
    scores = jnp.concatenate([cache_scores, draft_scores], axis=-1)
    row_max = jnp.max(scores, axis=-1, keepdims=True)
    weights = jnp.exp(scores - row_max)
    probabilities = (weights / jnp.sum(weights, axis=-1, keepdims=True)).astype(jnp.bfloat16)
    all_values = jnp.concatenate([cache_values, value_blocks], axis=1)
    attn_heads = (
        jnp.einsum("rhjc,rchd->rjhd", probabilities, all_values, preferred_element_type=jnp.float32)
        .astype(jnp.bfloat16)
        .reshape(tok_rows, feat_dev)
    )
    attn_term = jnp.dot(attn_heads, w_out, preferred_element_type=jnp.float32)
    swap = [(0, 1), (1, 0)]
    column_groups = model_width // (2 * slice_width)
    attn_blocks = attn_term.reshape(tok_rows, column_groups, 2, slice_width)
    kept = lax.dynamic_index_in_dim(attn_blocks, tc, axis=2, keepdims=False)
    given = lax.dynamic_index_in_dim(attn_blocks, 1 - tc, axis=2, keepdims=False)
    chip_sum = kept + lax.ppermute(given, "tc", swap)
    hidden_blocks = hidden.astype(jnp.float32).reshape(tok_rows, column_groups, 2, slice_width)
    residual = lax.dynamic_index_in_dim(hidden_blocks, tc, axis=2, keepdims=False) + lax.psum(
        chip_sum, ("th", "tl")
    )
    own_squares = jnp.sum(residual * residual, axis=(1, 2))
    all_squares = own_squares + lax.ppermute(own_squares, "tc", swap)
    gain_here = lax.dynamic_index_in_dim(
        moe_gain.reshape(column_groups, 2, slice_width), tc, axis=1, keepdims=False
    )
    normed_half = (
        residual * lax.rsqrt(all_squares / model_width + norm_eps)[:, None, None] * gain_here
    ).astype(jnp.bfloat16).reshape(tok_rows, column_groups * slice_width)
    residual_share = lax.dynamic_index_in_dim(
        residual, th * lax.axis_size("tl") + tl, axis=1, keepdims=False
    )
    experts_here = EXPERTS // req_count
    units_dev = w_down.shape[1]
    tok_ids = jnp.arange(tok_rows, dtype=jnp.int32)
    route_hot = (routes[:, :, None] == jnp.arange(EXPERTS, dtype=jnp.int32)).astype(jnp.float32)
    per_token = jnp.sum(route_hot, axis=1)
    weight_of = jnp.sum(route_weights[:, :, None] * route_hot, axis=1)
    earlier = (tok_ids[:, None] > tok_ids[None, :]).astype(jnp.bfloat16)
    slot_of = jnp.dot(earlier, per_token.astype(jnp.bfloat16), preferred_element_type=jnp.float32)
    capacity = CAP
    cap_ids = jnp.arange(capacity, dtype=jnp.float32)
    picked_here = lax.dynamic_index_in_dim(
        per_token.reshape(tok_rows, req_count, experts_here), th, axis=2, keepdims=False
    ).T
    slot_here = lax.dynamic_index_in_dim(
        slot_of.reshape(tok_rows, req_count, experts_here), th, axis=2, keepdims=False
    ).T
    select = jnp.where(
        (picked_here[:, None, :] > 0.5) & (slot_here[:, None, :] == cap_ids[None, :, None]), 1.0, 0.0
    ).astype(jnp.bfloat16)
    send_rows = jnp.einsum(
        "ict,tw->icw", select, normed_half, preferred_element_type=jnp.float32
    ).astype(jnp.bfloat16)
    received = lax.all_to_all(send_rows, "req", 0, 0, tiled=True)
    partner_rows = lax.ppermute(received, "tc", [(0, 1), (1, 0)])
    weight_blocks = w_gate_up[0].reshape(column_groups, 2, slice_width, 2, units_dev)
    own_weights = lax.dynamic_index_in_dim(weight_blocks, tc, axis=1, keepdims=False).reshape(
        model_width // 2, 2, units_dev
    )
    partner_weights = lax.dynamic_index_in_dim(
        weight_blocks, 1 - tc, axis=1, keepdims=False
    ).reshape(model_width // 2, 2, units_dev)
    gate_up = jnp.einsum(
        "scw,wgu->scgu", received, own_weights, preferred_element_type=jnp.float32
    ) + jnp.einsum(
        "scw,wgu->scgu", partner_rows, partner_weights, preferred_element_type=jnp.float32
    )
    activated = (jax.nn.silu(gate_up[..., 0, :]) * gate_up[..., 1, :]).astype(jnp.bfloat16)
    down = (
        w_down[0]
        .reshape(units_dev, 2, 2, 2, slice_width)
        .transpose(0, 3, 2, 1, 4)
        .reshape(units_dev, model_width)
    )
    partial = jnp.einsum(
        "scu,uw->scw", activated, down, preferred_element_type=jnp.float32
    ).astype(jnp.bfloat16)
    swap = [(0, 1), (1, 0)]
    half = model_width // 2
    kept = lax.dynamic_slice_in_dim(partial, tc * half, half, 2)
    given = lax.dynamic_slice_in_dim(partial, (1 - tc) * half, half, 2)
    pair_sum = kept.astype(jnp.float32) + lax.ppermute(given, "tc", swap).astype(jnp.float32)
    quarter = half // 2
    kept = lax.dynamic_slice_in_dim(pair_sum, tl * quarter, quarter, 2)
    given = lax.dynamic_slice_in_dim(pair_sum, (1 - tl) * quarter, quarter, 2).astype(jnp.bfloat16)
    quad_sum = (kept + lax.ppermute(given, "tl", swap).astype(jnp.float32)).astype(jnp.bfloat16)
    back = (
        quad_sum.reshape(req_count, capacity, 2, slice_width)
        .transpose(0, 2, 1, 3)
        .reshape(req_count * 2, capacity, slice_width)
    )
    returned = lax.all_to_all(back, ("req", "th"), 0, 0, tiled=True)
    combine = weight_of[:, :, None] * (slot_of[:, :, None] == cap_ids[None, None, :])
    mixture = jnp.dot(
        combine.reshape(tok_rows, EXPERTS * capacity),
        returned.reshape(EXPERTS * capacity, slice_width).astype(jnp.float32),
        precision=lax.Precision.HIGHEST,
        preferred_element_type=jnp.float32,
    )
    output = (residual_share + mixture).astype(jnp.bfloat16)
    picked_rows = (jnp.arange(req_local, dtype=jnp.int32)[:, None] * draft_len + accepted).reshape(
        -1
    )
    accepted_kv = jnp.stack(
        [keys_new.reshape(tok_rows, feat_dev)[picked_rows], values_new[picked_rows]]
    )
    return (output, accepted_kv)


def solution(mesh):
    req_count = mesh.shape["req"]
    devices = mesh.devices.reshape(req_count, 2, 2, mesh.shape["tp"] // 4)
    split_mesh = Mesh(devices, ("req",) + TP)
    return jax.shard_map(
        local,
        mesh=split_mesh,
        in_specs=(
            P("req", None),
            P(None, "req", None, TP),
            P("req", None),
            P("req"),
            P("req", None),
            P("req", None),
            P(),
            P(None, None, TP),
            P(None, TP),
            P(TP, None),
            P(),
            P("req", None),
            P("req", None),
            P("req", None, None, TP),
            P("req", TP, None),
        ),
        out_specs=(P("req", TP), P(None, "req", TP)),
        check_vma=False,
    )
```

```python
import jax
import jax.numpy as jnp
from jax import lax
from jax.sharding import Mesh, PartitionSpec as P

HD = 128
FFE = 1024
EXPERTS = 64
CAP = 40
TP = ("th", "tl", "tc")
SLOT_CHUNKS = 2


norm_eps = 1e-05
rope_base = 10000.0
masked_score = -1e30


def rms_scale(values, gain):
    return values * lax.rsqrt(jnp.mean(values * values, axis=-1, keepdims=True) + norm_eps) * gain


def tree_masks(parents):
    slot_count = parents.shape[-1]
    slot_ids = jnp.arange(slot_count, dtype=jnp.int32)
    parent_hot = (parents[..., :, None] == slot_ids).astype(jnp.float32)
    ancestry = jnp.minimum(jnp.eye(slot_count, dtype=jnp.float32) + parent_hot, 1.0)
    for squaring in range(slot_count.bit_length()):
        ancestry = jnp.minimum(
            jnp.einsum("rij,rjk->rik", ancestry, ancestry, precision=lax.Precision.HIGHEST), 1.0
        )
    depths = jnp.sum(ancestry, axis=-1).astype(jnp.int32) - 1
    return (ancestry, depths)


def rotate(values, positions):
    head_dim = values.shape[-1]
    half_dim = head_dim // 2
    frequency = rope_base ** (-jnp.arange(half_dim, dtype=jnp.float32) * 2.0 / head_dim)
    angles = positions.astype(jnp.float32)[:, None] * frequency[None, :]
    cosine = jnp.cos(angles)[:, None, :]
    sine_part = jnp.sin(angles)[:, None, :]
    first_half = values[..., :half_dim]
    second = values[..., half_dim:]
    return jnp.concatenate(
        [first_half * cosine - second * sine_part, second * cosine + first_half * sine_part],
        axis=-1,
    )


def local(
    hidden,
    kv_cache,
    page_table,
    cache_lens,
    parents,
    accepted,
    attn_gain,
    w_qkv,
    qk_gain,
    w_out,
    moe_gain,
    routes,
    route_weights,
    w_gate_up,
    w_down,
):
    tok_rows, model_width = hidden.shape
    th = lax.axis_index("th")
    tl = lax.axis_index("tl")
    tc = lax.axis_index("tc")
    tp_count = lax.axis_size(TP)
    req_count = lax.axis_size("req")
    slice_width = model_width // tp_count
    slice_start = ((th * lax.axis_size("tl") + tl) * lax.axis_size("tc") + tc) * slice_width
    req_local, draft_len = parents.shape
    feat_dev = w_qkv.shape[2]
    local_heads = feat_dev // HD
    ancestry, depths = tree_masks(parents)
    positions = (cache_lens[:, None] + depths).reshape(-1)
    normed_in = rms_scale(hidden.astype(jnp.float32), attn_gain).astype(jnp.bfloat16)
    projected = jnp.dot(
        normed_in, w_qkv.reshape(model_width, 3 * feat_dev), preferred_element_type=jnp.float32
    ).reshape(tok_rows, 3, feat_dev)
    query_raw = projected[:, 0]
    key_raw = projected[:, 1]
    values_new = projected[:, 2].astype(jnp.bfloat16)
    query_total, key_total = lax.psum(
        (jnp.sum(query_raw * query_raw, axis=-1), jnp.sum(key_raw * key_raw, axis=-1)), TP
    )
    query_normed = query_raw * lax.rsqrt(query_total[:, None] / model_width + norm_eps) * qk_gain[0]
    key_normed = key_raw * lax.rsqrt(key_total[:, None] / model_width + norm_eps) * qk_gain[1]
    query_rot = rotate(query_normed.reshape(tok_rows, local_heads, HD), positions).astype(
        jnp.bfloat16
    )
    keys_new = rotate(key_normed.reshape(tok_rows, local_heads, HD), positions).astype(jnp.bfloat16)
    page_rows = kv_cache[:, page_table.reshape(-1)]
    context = page_table.shape[1] * kv_cache.shape[2]
    cache_keys = page_rows[0].reshape(req_local, context, local_heads, HD)
    cache_values = page_rows[1].reshape(req_local, context, local_heads, HD)
    query_blocks = query_rot.reshape(req_local, draft_len, local_heads, HD)
    key_blocks = keys_new.reshape(req_local, draft_len, local_heads, HD)
    value_blocks = values_new.reshape(req_local, draft_len, local_heads, HD)
    score_scale = HD ** (-0.5)
    cache_scores = (
        jnp.einsum("rjhd,rchd->rhjc", query_blocks, cache_keys, preferred_element_type=jnp.float32)
        * score_scale
    )
    live_keys = jnp.arange(context, dtype=jnp.int32)[None, :] < cache_lens[:, None]
    cache_scores = jnp.where(live_keys[:, None, None, :], cache_scores, masked_score)
    draft_scores = (
        jnp.einsum("rjhd,rihd->rhji", query_blocks, key_blocks, preferred_element_type=jnp.float32)
        * score_scale
    )
    draft_scores = jnp.where(ancestry[:, None, :, :] > 0.5, draft_scores, masked_score)
    scores = jnp.concatenate([cache_scores, draft_scores], axis=-1)
    row_max = jnp.max(scores, axis=-1, keepdims=True)
    weights = jnp.exp(scores - row_max)
    probabilities = (weights / jnp.sum(weights, axis=-1, keepdims=True)).astype(jnp.bfloat16)
    all_values = jnp.concatenate([cache_values, value_blocks], axis=1)
    attn_heads = (
        jnp.einsum("rhjc,rchd->rjhd", probabilities, all_values, preferred_element_type=jnp.float32)
        .astype(jnp.bfloat16)
        .reshape(tok_rows, feat_dev)
    )
    attn_term = jnp.dot(attn_heads, w_out, preferred_element_type=jnp.float32)
    swap = [(0, 1), (1, 0)]
    column_groups = model_width // (2 * slice_width)
    attn_blocks = attn_term.reshape(tok_rows, column_groups, 2, slice_width)
    kept = lax.dynamic_index_in_dim(attn_blocks, tc, axis=2, keepdims=False)
    given = lax.dynamic_index_in_dim(attn_blocks, 1 - tc, axis=2, keepdims=False)
    chip_sum = kept + lax.ppermute(given, "tc", swap)
    hidden_blocks = hidden.astype(jnp.float32).reshape(tok_rows, column_groups, 2, slice_width)
    residual = lax.dynamic_index_in_dim(hidden_blocks, tc, axis=2, keepdims=False) + lax.psum(
        chip_sum, ("th", "tl")
    )
    own_squares = jnp.sum(residual * residual, axis=(1, 2))
    all_squares = own_squares + lax.ppermute(own_squares, "tc", swap)
    gain_here = lax.dynamic_index_in_dim(
        moe_gain.reshape(column_groups, 2, slice_width), tc, axis=1, keepdims=False
    )
    normed_half = (
        residual * lax.rsqrt(all_squares / model_width + norm_eps)[:, None, None] * gain_here
    ).astype(jnp.bfloat16).reshape(tok_rows, column_groups * slice_width)
    residual_share = lax.dynamic_index_in_dim(
        residual, th * lax.axis_size("tl") + tl, axis=1, keepdims=False
    )
    experts_here = EXPERTS // req_count
    units_dev = w_down.shape[1]
    tok_ids = jnp.arange(tok_rows, dtype=jnp.int32)
    route_hot = (routes[:, :, None] == jnp.arange(EXPERTS, dtype=jnp.int32)).astype(jnp.float32)
    per_token = jnp.sum(route_hot, axis=1)
    weight_of = jnp.sum(route_weights[:, :, None] * route_hot, axis=1)
    earlier = (tok_ids[:, None] > tok_ids[None, :]).astype(jnp.bfloat16)
    slot_of = jnp.dot(earlier, per_token.astype(jnp.bfloat16), preferred_element_type=jnp.float32)
    capacity = CAP
    cap_ids = jnp.arange(capacity, dtype=jnp.float32)
    picked_here = lax.dynamic_index_in_dim(
        per_token.reshape(tok_rows, req_count, experts_here), th, axis=2, keepdims=False
    ).T
    slot_here = lax.dynamic_index_in_dim(
        slot_of.reshape(tok_rows, req_count, experts_here), th, axis=2, keepdims=False
    ).T
    select = jnp.where(
        (picked_here[:, None, :] > 0.5) & (slot_here[:, None, :] == cap_ids[None, :, None]), 1.0, 0.0
    ).astype(jnp.bfloat16)
    weight_blocks = w_gate_up[0].reshape(column_groups, 2, slice_width, 2, units_dev)
    own_weights = lax.dynamic_index_in_dim(weight_blocks, tc, axis=1, keepdims=False).reshape(
        model_width // 2, 2, units_dev
    )
    partner_weights = lax.dynamic_index_in_dim(
        weight_blocks, 1 - tc, axis=1, keepdims=False
    ).reshape(model_width // 2, 2, units_dev)
    down = (
        w_down[0]
        .reshape(units_dev, 2, 2, 2, slice_width)
        .transpose(0, 3, 2, 1, 4)
        .reshape(units_dev, model_width)
    )
    swap = [(0, 1), (1, 0)]
    half = model_width // 2
    quarter = half // 2
    chunk_slots = capacity // SLOT_CHUNKS
    returned_parts = []
    for chunk in range(SLOT_CHUNKS):
        select_part = select[:, chunk * chunk_slots : (chunk + 1) * chunk_slots]
        send_rows = jnp.einsum(
            "ict,tw->icw", select_part, normed_half, preferred_element_type=jnp.float32
        ).astype(jnp.bfloat16)
        received = lax.all_to_all(send_rows, "req", 0, 0, tiled=True)
        partner_rows = lax.ppermute(received, "tc", swap)
        gate_up = jnp.einsum(
            "scw,wgu->scgu", received, own_weights, preferred_element_type=jnp.float32
        ) + jnp.einsum(
            "scw,wgu->scgu", partner_rows, partner_weights, preferred_element_type=jnp.float32
        )
        activated = (jax.nn.silu(gate_up[..., 0, :]) * gate_up[..., 1, :]).astype(jnp.bfloat16)
        partial = jnp.einsum(
            "scu,uw->scw", activated, down, preferred_element_type=jnp.float32
        ).astype(jnp.bfloat16)
        kept = lax.dynamic_slice_in_dim(partial, tc * half, half, 2)
        given = lax.dynamic_slice_in_dim(partial, (1 - tc) * half, half, 2)
        pair_sum = kept.astype(jnp.float32) + lax.ppermute(given, "tc", swap).astype(jnp.float32)
        kept = lax.dynamic_slice_in_dim(pair_sum, tl * quarter, quarter, 2)
        given = lax.dynamic_slice_in_dim(pair_sum, (1 - tl) * quarter, quarter, 2).astype(
            jnp.bfloat16
        )
        quad_sum = (kept + lax.ppermute(given, "tl", swap).astype(jnp.float32)).astype(
            jnp.bfloat16
        )
        back = (
            quad_sum.reshape(req_count, chunk_slots, 2, slice_width)
            .transpose(0, 2, 1, 3)
            .reshape(req_count * 2, chunk_slots, slice_width)
        )
        returned_parts.append(lax.all_to_all(back, ("req", "th"), 0, 0, tiled=True))
    returned = jnp.concatenate(returned_parts, axis=1)
    combine = weight_of[:, :, None] * (slot_of[:, :, None] == cap_ids[None, None, :])
    mixture = jnp.dot(
        combine.reshape(tok_rows, EXPERTS * capacity),
        returned.reshape(EXPERTS * capacity, slice_width).astype(jnp.float32),
        precision=lax.Precision.HIGHEST,
        preferred_element_type=jnp.float32,
    )
    output = (residual_share + mixture).astype(jnp.bfloat16)
    picked_rows = (jnp.arange(req_local, dtype=jnp.int32)[:, None] * draft_len + accepted).reshape(
        -1
    )
    accepted_kv = jnp.stack(
        [keys_new.reshape(tok_rows, feat_dev)[picked_rows], values_new[picked_rows]]
    )
    return (output, accepted_kv)


def solution(mesh):
    req_count = mesh.shape["req"]
    devices = mesh.devices.reshape(req_count, 2, 2, mesh.shape["tp"] // 4)
    split_mesh = Mesh(devices, ("req",) + TP)
    return jax.shard_map(
        local,
        mesh=split_mesh,
        in_specs=(
            P("req", None),
            P(None, "req", None, TP),
            P("req", None),
            P("req"),
            P("req", None),
            P("req", None),
            P(),
            P(None, None, TP),
            P(None, TP),
            P(TP, None),
            P(),
            P("req", None),
            P("req", None),
            P("req", None, None, TP),
            P("req", TP, None),
        ),
        out_specs=(P("req", TP), P(None, "req", TP)),
        check_vma=False,
    )
```

```python
import jax
import jax.numpy as jnp
from jax import lax
from jax.sharding import Mesh, PartitionSpec as P

HD = 128
FFE = 1024
EXPERTS = 64
CAP = 40
TP = ("th", "tl", "tc")


norm_eps = 1e-05
rope_base = 10000.0
masked_score = -1e30


def rms_scale(values, gain):
    return values * lax.rsqrt(jnp.mean(values * values, axis=-1, keepdims=True) + norm_eps) * gain


def tree_masks(parents):
    slot_count = parents.shape[-1]
    slot_ids = jnp.arange(slot_count, dtype=jnp.int32)
    parent_hot = (parents[..., :, None] == slot_ids).astype(jnp.float32)
    ancestry = jnp.minimum(jnp.eye(slot_count, dtype=jnp.float32) + parent_hot, 1.0)
    for squaring in range(slot_count.bit_length()):
        ancestry = jnp.minimum(
            jnp.einsum("rij,rjk->rik", ancestry, ancestry, precision=lax.Precision.HIGHEST), 1.0
        )
    depths = jnp.sum(ancestry, axis=-1).astype(jnp.int32) - 1
    return (ancestry, depths)


def rotate(values, positions):
    head_dim = values.shape[-1]
    half_dim = head_dim // 2
    frequency = rope_base ** (-jnp.arange(half_dim, dtype=jnp.float32) * 2.0 / head_dim)
    angles = positions.astype(jnp.float32)[:, None] * frequency[None, :]
    cosine = jnp.cos(angles)[:, None, :]
    sine_part = jnp.sin(angles)[:, None, :]
    first_half = values[..., :half_dim]
    second = values[..., half_dim:]
    return jnp.concatenate(
        [first_half * cosine - second * sine_part, second * cosine + first_half * sine_part],
        axis=-1,
    )


def local(
    hidden,
    kv_cache,
    page_table,
    cache_lens,
    parents,
    accepted,
    attn_gain,
    w_qkv,
    qk_gain,
    w_out,
    moe_gain,
    routes,
    route_weights,
    w_gate_up,
    w_down,
):
    tok_rows, model_width = hidden.shape
    th = lax.axis_index("th")
    tl = lax.axis_index("tl")
    tc = lax.axis_index("tc")
    tp_count = lax.axis_size(TP)
    req_count = lax.axis_size("req")
    slice_width = model_width // tp_count
    slice_start = ((th * lax.axis_size("tl") + tl) * lax.axis_size("tc") + tc) * slice_width
    req_local, draft_len = parents.shape
    feat_dev = w_qkv.shape[2]
    local_heads = feat_dev // HD
    ancestry, depths = tree_masks(parents)
    positions = (cache_lens[:, None] + depths).reshape(-1)
    normed_in = rms_scale(hidden.astype(jnp.float32), attn_gain).astype(jnp.bfloat16)
    projected = jnp.einsum(
        "tw,wgf->tgf", normed_in, w_qkv, preferred_element_type=jnp.float32
    )
    query_raw = projected[:, 0]
    key_raw = projected[:, 1]
    values_new = projected[:, 2].astype(jnp.bfloat16)
    swap = [(0, 1), (1, 0)]
    squares = jnp.stack(
        [jnp.sum(query_raw * query_raw, axis=-1), jnp.sum(key_raw * key_raw, axis=-1)]
    )
    squares = squares + lax.ppermute(squares, "tc", swap)
    squares = squares + lax.ppermute(squares, "tl", swap)
    squares = squares + lax.ppermute(squares, "th", swap)
    query_normed = query_raw * lax.rsqrt(squares[0][:, None] / model_width + norm_eps) * qk_gain[0]
    key_normed = key_raw * lax.rsqrt(squares[1][:, None] / model_width + norm_eps) * qk_gain[1]
    query_rot = rotate(query_normed.reshape(tok_rows, local_heads, HD), positions).astype(
        jnp.bfloat16
    )
    keys_new = rotate(key_normed.reshape(tok_rows, local_heads, HD), positions).astype(jnp.bfloat16)
    local_pages, page_len = kv_cache.shape[1], kv_cache.shape[2]
    all_keys = kv_cache[0].reshape(local_pages * page_len, feat_dev)
    all_values = kv_cache[1].reshape(local_pages * page_len, feat_dev)
    page_ids = jnp.arange(local_pages, dtype=jnp.int32)
    page_match = (page_table[:, :, None] == page_ids[None, None, :]).astype(jnp.int32)
    page_owned = jnp.sum(page_match, axis=1)
    page_start = jnp.sum(
        page_match * (jnp.arange(page_table.shape[1], dtype=jnp.int32) * page_len)[None, :, None],
        axis=1,
    )
    key_pos = (page_start[:, :, None] + jnp.arange(page_len, dtype=jnp.int32)[None, None, :]).reshape(
        req_local, local_pages * page_len
    )
    live_keys = (jnp.repeat(page_owned, page_len, axis=1) > 0) & (key_pos < cache_lens[:, None])
    score_scale = HD ** (-0.5)
    head_outputs = []
    for head in range(local_heads):
        lanes = slice(head * HD, (head + 1) * HD)
        queries = query_rot[:, head].reshape(req_local, draft_len, HD)
        own_keys = keys_new[:, head].reshape(req_local, draft_len, HD)
        own_values = values_new[:, lanes].reshape(req_local, draft_len, HD)
        cache_scores = (
            jnp.einsum(
                "rjd,cd->rjc", queries, all_keys[:, lanes], preferred_element_type=jnp.float32
            )
            * score_scale
        )
        cache_scores = jnp.where(live_keys[:, None, :], cache_scores, masked_score)
        draft_scores = (
            jnp.einsum("rjd,rid->rji", queries, own_keys, preferred_element_type=jnp.float32)
            * score_scale
        )
        draft_scores = jnp.where(ancestry > 0.5, draft_scores, masked_score)
        row_max = jnp.maximum(
            jnp.max(cache_scores, axis=-1, keepdims=True),
            jnp.max(draft_scores, axis=-1, keepdims=True),
        )
        cache_weights = jnp.exp(cache_scores - row_max)
        draft_weights = jnp.exp(draft_scores - row_max)
        total = jnp.sum(cache_weights, axis=-1, keepdims=True) + jnp.sum(
            draft_weights, axis=-1, keepdims=True
        )
        cache_probs = (cache_weights / total).astype(jnp.bfloat16)
        draft_probs = (draft_weights / total).astype(jnp.bfloat16)
        mixed = jnp.einsum(
            "rjc,cd->rjd", cache_probs, all_values[:, lanes], preferred_element_type=jnp.float32
        ) + jnp.einsum("rji,rid->rjd", draft_probs, own_values, preferred_element_type=jnp.float32)
        head_outputs.append(mixed.astype(jnp.bfloat16).reshape(tok_rows, HD))
    attn_heads = jnp.concatenate(head_outputs, axis=1)
    attn_term = jnp.dot(attn_heads, w_out, preferred_element_type=jnp.float32)
    column_groups = model_width // (2 * slice_width)
    attn_blocks = attn_term.reshape(tok_rows, column_groups, 2, slice_width)
    kept = lax.dynamic_index_in_dim(attn_blocks, tc, axis=2, keepdims=False)
    given = lax.dynamic_index_in_dim(attn_blocks, 1 - tc, axis=2, keepdims=False)
    chip_sum = kept + lax.ppermute(given, "tc", swap)
    hidden_blocks = hidden.astype(jnp.float32).reshape(tok_rows, column_groups, 2, slice_width)
    residual = lax.dynamic_index_in_dim(hidden_blocks, tc, axis=2, keepdims=False) + lax.psum(
        chip_sum, ("th", "tl")
    )
    own_squares = jnp.sum(residual * residual, axis=(1, 2))
    all_squares = own_squares + lax.ppermute(own_squares, "tc", swap)
    gain_here = lax.dynamic_index_in_dim(
        moe_gain.reshape(column_groups, 2, slice_width), tc, axis=1, keepdims=False
    )
    normed_half = (
        residual * lax.rsqrt(all_squares / model_width + norm_eps)[:, None, None] * gain_here
    ).astype(jnp.bfloat16).reshape(tok_rows, column_groups * slice_width)
    residual_share = lax.dynamic_index_in_dim(
        residual, th * lax.axis_size("tl") + tl, axis=1, keepdims=False
    )
    experts_here = EXPERTS // req_count
    units_dev = w_down.shape[1]
    tok_ids = jnp.arange(tok_rows, dtype=jnp.int32)
    route_hot = (routes[:, :, None] == jnp.arange(EXPERTS, dtype=jnp.int32)).astype(jnp.float32)
    per_token = jnp.sum(route_hot, axis=1)
    weight_of = jnp.sum(route_weights[:, :, None] * route_hot, axis=1)
    earlier = (tok_ids[:, None] > tok_ids[None, :]).astype(jnp.bfloat16)
    slot_of = jnp.dot(earlier, per_token.astype(jnp.bfloat16), preferred_element_type=jnp.float32)
    capacity = CAP
    cap_ids = jnp.arange(capacity, dtype=jnp.float32)
    picked_here = lax.dynamic_index_in_dim(
        per_token.reshape(tok_rows, req_count, experts_here), th, axis=2, keepdims=False
    ).T
    slot_here = lax.dynamic_index_in_dim(
        slot_of.reshape(tok_rows, req_count, experts_here), th, axis=2, keepdims=False
    ).T
    select = jnp.where(
        (picked_here[:, None, :] > 0.5) & (slot_here[:, None, :] == cap_ids[None, :, None]), 1.0, 0.0
    ).astype(jnp.bfloat16)
    send_rows = jnp.einsum(
        "ict,tw->icw", select, normed_half, preferred_element_type=jnp.float32
    ).astype(jnp.bfloat16)
    received = lax.all_to_all(send_rows, "req", 0, 0, tiled=True)
    partner_rows = lax.ppermute(received, "tc", [(0, 1), (1, 0)])
    weight_blocks = w_gate_up[0].reshape(column_groups, 2, slice_width, 2, units_dev)
    own_weights = lax.dynamic_index_in_dim(weight_blocks, tc, axis=1, keepdims=False).reshape(
        model_width // 2, 2, units_dev
    )
    partner_weights = lax.dynamic_index_in_dim(
        weight_blocks, 1 - tc, axis=1, keepdims=False
    ).reshape(model_width // 2, 2, units_dev)
    gate_up = jnp.einsum(
        "scw,wgu->scgu", received, own_weights, preferred_element_type=jnp.float32
    ) + jnp.einsum(
        "scw,wgu->scgu", partner_rows, partner_weights, preferred_element_type=jnp.float32
    )
    activated = (jax.nn.silu(gate_up[..., 0, :]) * gate_up[..., 1, :]).astype(jnp.bfloat16)
    down = (
        w_down[0]
        .reshape(units_dev, 2, 2, 2, slice_width)
        .transpose(0, 3, 2, 1, 4)
        .reshape(units_dev, model_width)
    )
    partial = jnp.einsum(
        "scu,uw->scw", activated, down, preferred_element_type=jnp.float32
    ).astype(jnp.bfloat16)
    swap = [(0, 1), (1, 0)]
    half = model_width // 2
    kept = lax.dynamic_slice_in_dim(partial, tc * half, half, 2)
    given = lax.dynamic_slice_in_dim(partial, (1 - tc) * half, half, 2)
    pair_sum = kept.astype(jnp.float32) + lax.ppermute(given, "tc", swap).astype(jnp.float32)
    quarter = half // 2
    kept = lax.dynamic_slice_in_dim(pair_sum, tl * quarter, quarter, 2)
    given = lax.dynamic_slice_in_dim(pair_sum, (1 - tl) * quarter, quarter, 2).astype(jnp.bfloat16)
    quad_sum = (kept + lax.ppermute(given, "tl", swap).astype(jnp.float32)).astype(jnp.bfloat16)
    back = (
        quad_sum.reshape(req_count, capacity, 2, slice_width)
        .transpose(0, 2, 1, 3)
        .reshape(req_count * 2, capacity, slice_width)
    )
    returned = lax.all_to_all(back, ("req", "th"), 0, 0, tiled=True)
    combine = weight_of[:, :, None] * (slot_of[:, :, None] == cap_ids[None, None, :])
    mixture = jnp.dot(
        combine.reshape(tok_rows, EXPERTS * capacity),
        returned.reshape(EXPERTS * capacity, slice_width).astype(jnp.float32),
        precision=lax.Precision.HIGHEST,
        preferred_element_type=jnp.float32,
    )
    output = (residual_share + mixture).astype(jnp.bfloat16)
    picked_rows = (jnp.arange(req_local, dtype=jnp.int32)[:, None] * draft_len + accepted).reshape(
        -1
    )
    accepted_kv = jnp.stack(
        [keys_new.reshape(tok_rows, feat_dev)[picked_rows], values_new[picked_rows]]
    )
    return (output, accepted_kv)


def solution(mesh):
    req_count = mesh.shape["req"]
    devices = mesh.devices.reshape(req_count, 2, 2, mesh.shape["tp"] // 4)
    split_mesh = Mesh(devices, ("req",) + TP)
    return jax.shard_map(
        local,
        mesh=split_mesh,
        in_specs=(
            P("req", None),
            P(None, "req", None, TP),
            P("req", None),
            P("req"),
            P("req", None),
            P("req", None),
            P(),
            P(None, None, TP),
            P(None, TP),
            P(TP, None),
            P(),
            P("req", None),
            P("req", None),
            P("req", None, None, TP),
            P("req", TP, None),
        ),
        out_specs=(P("req", TP), P(None, "req", TP)),
        check_vma=False,
    )
```

```python
import jax
import jax.numpy as jnp
from jax import lax
from jax.sharding import Mesh, PartitionSpec as P

HD = 128
FFE = 1024
EXPERTS = 64
CAP = 40
TP = ("th", "tl", "tc")


norm_eps = 1e-05
rope_base = 10000.0
masked_score = -1e30


def rms_scale(values, gain):
    return values * lax.rsqrt(jnp.mean(values * values, axis=-1, keepdims=True) + norm_eps) * gain


def tree_masks(parents):
    slot_count = parents.shape[-1]
    slot_ids = jnp.arange(slot_count, dtype=jnp.int32)
    parent_hot = (parents[..., :, None] == slot_ids).astype(jnp.float32)
    ancestry = jnp.minimum(jnp.eye(slot_count, dtype=jnp.float32) + parent_hot, 1.0)
    for squaring in range(slot_count.bit_length()):
        ancestry = jnp.minimum(
            jnp.einsum("rij,rjk->rik", ancestry, ancestry, precision=lax.Precision.HIGHEST), 1.0
        )
    depths = jnp.sum(ancestry, axis=-1).astype(jnp.int32) - 1
    return (ancestry, depths)


def rotate(values, positions):
    head_dim = values.shape[-1]
    half_dim = head_dim // 2
    frequency = rope_base ** (-jnp.arange(half_dim, dtype=jnp.float32) * 2.0 / head_dim)
    angles = positions.astype(jnp.float32)[:, None] * frequency[None, :]
    cosine = jnp.cos(angles)[:, None, :]
    sine_part = jnp.sin(angles)[:, None, :]
    first_half = values[..., :half_dim]
    second = values[..., half_dim:]
    return jnp.concatenate(
        [first_half * cosine - second * sine_part, second * cosine + first_half * sine_part],
        axis=-1,
    )


def local(
    hidden,
    kv_cache,
    page_table,
    cache_lens,
    parents,
    accepted,
    attn_gain,
    w_qkv,
    qk_gain,
    w_out,
    moe_gain,
    routes,
    route_weights,
    w_gate_up,
    w_down,
):
    tok_rows, model_width = hidden.shape
    th = lax.axis_index("th")
    tl = lax.axis_index("tl")
    tc = lax.axis_index("tc")
    tp_count = lax.axis_size(TP)
    req_count = lax.axis_size("req")
    slice_width = model_width // tp_count
    slice_start = ((th * lax.axis_size("tl") + tl) * lax.axis_size("tc") + tc) * slice_width
    req_local, draft_len = parents.shape
    feat_dev = w_qkv.shape[2]
    local_heads = feat_dev // HD
    ancestry, depths = tree_masks(parents)
    positions = (cache_lens[:, None] + depths).reshape(-1)
    normed_in = rms_scale(hidden.astype(jnp.float32), attn_gain).astype(jnp.bfloat16)
    projected = jnp.einsum(
        "tw,wgf->tgf", normed_in, w_qkv, preferred_element_type=jnp.float32
    )
    query_raw = projected[:, 0]
    key_raw = projected[:, 1]
    values_new = projected[:, 2].astype(jnp.bfloat16)
    swap = [(0, 1), (1, 0)]
    squares = jnp.stack(
        [jnp.sum(query_raw * query_raw, axis=-1), jnp.sum(key_raw * key_raw, axis=-1)]
    )
    squares = squares + lax.ppermute(squares, "tc", swap)
    squares = squares + lax.ppermute(squares, "tl", swap)
    squares = squares + lax.ppermute(squares, "th", swap)
    query_normed = query_raw * lax.rsqrt(squares[0][:, None] / model_width + norm_eps) * qk_gain[0]
    key_normed = key_raw * lax.rsqrt(squares[1][:, None] / model_width + norm_eps) * qk_gain[1]
    query_rot = rotate(query_normed.reshape(tok_rows, local_heads, HD), positions).astype(
        jnp.bfloat16
    )
    keys_new = rotate(key_normed.reshape(tok_rows, local_heads, HD), positions).astype(jnp.bfloat16)
    local_pages, page_len = kv_cache.shape[1], kv_cache.shape[2]
    all_keys = kv_cache[0].reshape(local_pages * page_len, feat_dev)
    all_values = kv_cache[1].reshape(local_pages * page_len, feat_dev)
    page_ids = jnp.arange(local_pages, dtype=jnp.int32)
    page_match = (page_table[:, :, None] == page_ids[None, None, :]).astype(jnp.int32)
    page_owned = jnp.sum(page_match, axis=1)
    page_start = jnp.sum(
        page_match * (jnp.arange(page_table.shape[1], dtype=jnp.int32) * page_len)[None, :, None],
        axis=1,
    )
    key_pos = (page_start[:, :, None] + jnp.arange(page_len, dtype=jnp.int32)[None, None, :]).reshape(
        req_local, local_pages * page_len
    )
    live_keys = (jnp.repeat(page_owned, page_len, axis=1) > 0) & (key_pos < cache_lens[:, None])
    score_scale = HD ** (-0.5)
    head_outputs = []
    for head in range(local_heads):
        lanes = slice(head * HD, (head + 1) * HD)
        queries = query_rot[:, head].reshape(req_local, draft_len, HD)
        own_keys = keys_new[:, head].reshape(req_local, draft_len, HD)
        own_values = values_new[:, lanes].reshape(req_local, draft_len, HD)
        cache_scores = (
            jnp.einsum(
                "rjd,cd->rjc", queries, all_keys[:, lanes], preferred_element_type=jnp.float32
            )
            * score_scale
        )
        cache_scores = jnp.where(live_keys[:, None, :], cache_scores, masked_score)
        draft_scores = (
            jnp.einsum("rjd,rid->rji", queries, own_keys, preferred_element_type=jnp.float32)
            * score_scale
        )
        draft_scores = jnp.where(ancestry > 0.5, draft_scores, masked_score)
        row_max = jnp.maximum(
            jnp.max(cache_scores, axis=-1, keepdims=True),
            jnp.max(draft_scores, axis=-1, keepdims=True),
        )
        cache_weights = jnp.exp(cache_scores - row_max)
        draft_weights = jnp.exp(draft_scores - row_max)
        total = jnp.sum(cache_weights, axis=-1, keepdims=True) + jnp.sum(
            draft_weights, axis=-1, keepdims=True
        )
        cache_probs = (cache_weights / total).astype(jnp.bfloat16)
        draft_probs = (draft_weights / total).astype(jnp.bfloat16)
        mixed = jnp.einsum(
            "rjc,cd->rjd", cache_probs, all_values[:, lanes], preferred_element_type=jnp.float32
        ) + jnp.einsum("rji,rid->rjd", draft_probs, own_values, preferred_element_type=jnp.float32)
        head_outputs.append(mixed.astype(jnp.bfloat16).reshape(tok_rows, HD))
    attn_heads = jnp.concatenate(head_outputs, axis=1)
    attn_term = jnp.dot(attn_heads, w_out, preferred_element_type=jnp.float32)
    column_groups = model_width // (2 * slice_width)
    attn_blocks = attn_term.reshape(tok_rows, column_groups, 2, slice_width)
    kept = lax.dynamic_index_in_dim(attn_blocks, tc, axis=2, keepdims=False)
    given = lax.dynamic_index_in_dim(attn_blocks, 1 - tc, axis=2, keepdims=False)
    chip_sum = kept + lax.ppermute(given, "tc", swap)
    hidden_blocks = hidden.astype(jnp.float32).reshape(tok_rows, column_groups, 2, slice_width)
    pair_blocks = chip_sum.reshape(tok_rows, column_groups // 2, 2, slice_width)
    row_sum = lax.dynamic_index_in_dim(pair_blocks, tl, axis=2, keepdims=False) + lax.ppermute(
        lax.dynamic_index_in_dim(pair_blocks, 1 - tl, axis=2, keepdims=False), "tl", swap
    )
    block_sum = lax.dynamic_index_in_dim(row_sum, th, axis=1, keepdims=False) + lax.ppermute(
        lax.dynamic_index_in_dim(row_sum, 1 - th, axis=1, keepdims=False), "th", swap
    )
    block_other = lax.ppermute(block_sum, "th", swap)
    row_sum = jnp.where(
        th == 0,
        jnp.stack([block_sum, block_other], axis=1),
        jnp.stack([block_other, block_sum], axis=1),
    )
    row_other = lax.ppermute(row_sum, "tl", swap)
    full_sum = jnp.where(
        tl == 0,
        jnp.stack([row_sum, row_other], axis=2),
        jnp.stack([row_other, row_sum], axis=2),
    ).reshape(tok_rows, column_groups, slice_width)
    residual = lax.dynamic_index_in_dim(hidden_blocks, tc, axis=2, keepdims=False) + full_sum
    own_squares = jnp.sum(residual * residual, axis=(1, 2))
    all_squares = own_squares + lax.ppermute(own_squares, "tc", swap)
    gain_here = lax.dynamic_index_in_dim(
        moe_gain.reshape(column_groups, 2, slice_width), tc, axis=1, keepdims=False
    )
    normed_half = (
        residual * lax.rsqrt(all_squares / model_width + norm_eps)[:, None, None] * gain_here
    ).astype(jnp.bfloat16).reshape(tok_rows, column_groups * slice_width)
    residual_share = lax.dynamic_index_in_dim(
        residual, th * lax.axis_size("tl") + tl, axis=1, keepdims=False
    )
    experts_here = EXPERTS // req_count
    units_dev = w_down.shape[1]
    tok_ids = jnp.arange(tok_rows, dtype=jnp.int32)
    route_hot = (routes[:, :, None] == jnp.arange(EXPERTS, dtype=jnp.int32)).astype(jnp.float32)
    per_token = jnp.sum(route_hot, axis=1)
    weight_of = jnp.sum(route_weights[:, :, None] * route_hot, axis=1)
    earlier = (tok_ids[:, None] > tok_ids[None, :]).astype(jnp.bfloat16)
    slot_of = jnp.dot(earlier, per_token.astype(jnp.bfloat16), preferred_element_type=jnp.float32)
    capacity = CAP
    cap_ids = jnp.arange(capacity, dtype=jnp.float32)
    picked_here = lax.dynamic_index_in_dim(
        per_token.reshape(tok_rows, req_count, experts_here), th, axis=2, keepdims=False
    ).T
    slot_here = lax.dynamic_index_in_dim(
        slot_of.reshape(tok_rows, req_count, experts_here), th, axis=2, keepdims=False
    ).T
    select = jnp.where(
        (picked_here[:, None, :] > 0.5) & (slot_here[:, None, :] == cap_ids[None, :, None]), 1.0, 0.0
    ).astype(jnp.bfloat16)
    send_rows = jnp.einsum(
        "ict,tw->icw", select, normed_half, preferred_element_type=jnp.float32
    ).astype(jnp.bfloat16)
    received = lax.all_to_all(send_rows, "req", 0, 0, tiled=True)
    partner_rows = lax.ppermute(received, "tc", [(0, 1), (1, 0)])
    weight_blocks = w_gate_up[0].reshape(column_groups, 2, slice_width, 2, units_dev)
    own_weights = lax.dynamic_index_in_dim(weight_blocks, tc, axis=1, keepdims=False).reshape(
        model_width // 2, 2, units_dev
    )
    partner_weights = lax.dynamic_index_in_dim(
        weight_blocks, 1 - tc, axis=1, keepdims=False
    ).reshape(model_width // 2, 2, units_dev)
    gate_up = jnp.einsum(
        "scw,wgu->scgu", received, own_weights, preferred_element_type=jnp.float32
    ) + jnp.einsum(
        "scw,wgu->scgu", partner_rows, partner_weights, preferred_element_type=jnp.float32
    )
    activated = (jax.nn.silu(gate_up[..., 0, :]) * gate_up[..., 1, :]).astype(jnp.bfloat16)
    down = (
        w_down[0]
        .reshape(units_dev, 2, 2, 2, slice_width)
        .transpose(0, 3, 2, 1, 4)
        .reshape(units_dev, model_width)
    )
    partial = jnp.einsum(
        "scu,uw->scw", activated, down, preferred_element_type=jnp.float32
    ).astype(jnp.bfloat16)
    swap = [(0, 1), (1, 0)]
    half = model_width // 2
    kept = lax.dynamic_slice_in_dim(partial, tc * half, half, 2)
    given = lax.dynamic_slice_in_dim(partial, (1 - tc) * half, half, 2)
    pair_sum = kept.astype(jnp.float32) + lax.ppermute(given, "tc", swap).astype(jnp.float32)
    quarter = half // 2
    kept = lax.dynamic_slice_in_dim(pair_sum, tl * quarter, quarter, 2)
    given = lax.dynamic_slice_in_dim(pair_sum, (1 - tl) * quarter, quarter, 2).astype(jnp.bfloat16)
    quad_sum = (kept + lax.ppermute(given, "tl", swap).astype(jnp.float32)).astype(jnp.bfloat16)
    back = (
        quad_sum.reshape(req_count, capacity, 2, slice_width)
        .transpose(0, 2, 1, 3)
        .reshape(req_count * 2, capacity, slice_width)
    )
    returned = lax.all_to_all(back, ("req", "th"), 0, 0, tiled=True)
    combine = weight_of[:, :, None] * (slot_of[:, :, None] == cap_ids[None, None, :])
    mixture = jnp.dot(
        combine.reshape(tok_rows, EXPERTS * capacity),
        returned.reshape(EXPERTS * capacity, slice_width).astype(jnp.float32),
        precision=lax.Precision.HIGHEST,
        preferred_element_type=jnp.float32,
    )
    output = (residual_share + mixture).astype(jnp.bfloat16)
    picked_rows = (jnp.arange(req_local, dtype=jnp.int32)[:, None] * draft_len + accepted).reshape(
        -1
    )
    accepted_kv = jnp.stack(
        [keys_new.reshape(tok_rows, feat_dev)[picked_rows], values_new[picked_rows]]
    )
    return (output, accepted_kv)


def solution(mesh):
    req_count = mesh.shape["req"]
    devices = mesh.devices.reshape(req_count, 2, 2, mesh.shape["tp"] // 4)
    split_mesh = Mesh(devices, ("req",) + TP)
    return jax.shard_map(
        local,
        mesh=split_mesh,
        in_specs=(
            P("req", None),
            P(None, "req", None, TP),
            P("req", None),
            P("req"),
            P("req", None),
            P("req", None),
            P(),
            P(None, None, TP),
            P(None, TP),
            P(TP, None),
            P(),
            P("req", None),
            P("req", None),
            P("req", None, None, TP),
            P("req", TP, None),
        ),
        out_specs=(P("req", TP), P(None, "req", TP)),
        check_vma=False,
    )
```

```python
import jax
import jax.numpy as jnp
from jax import lax
from jax.sharding import Mesh, PartitionSpec as P

HD = 128
FFE = 1024
EXPERTS = 64
CAP = 40
TP = ("th", "tl", "tc")


norm_eps = 1e-05
rope_base = 10000.0
masked_score = -1e30


def rms_scale(values, gain):
    return values * lax.rsqrt(jnp.mean(values * values, axis=-1, keepdims=True) + norm_eps) * gain


def tree_masks(parents):
    slot_count = parents.shape[-1]
    slot_ids = jnp.arange(slot_count, dtype=jnp.int32)
    parent_hot = (parents[..., :, None] == slot_ids).astype(jnp.float32)
    ancestry = jnp.minimum(jnp.eye(slot_count, dtype=jnp.float32) + parent_hot, 1.0)
    for squaring in range(slot_count.bit_length()):
        ancestry = jnp.minimum(
            jnp.einsum("rij,rjk->rik", ancestry, ancestry, precision=lax.Precision.HIGHEST), 1.0
        )
    depths = jnp.sum(ancestry, axis=-1).astype(jnp.int32) - 1
    return (ancestry, depths)


def rotate(values, positions):
    head_dim = values.shape[-1]
    half_dim = head_dim // 2
    frequency = rope_base ** (-jnp.arange(half_dim, dtype=jnp.float32) * 2.0 / head_dim)
    angles = positions.astype(jnp.float32)[:, None] * frequency[None, :]
    cosine = jnp.cos(angles)[:, None, :]
    sine_part = jnp.sin(angles)[:, None, :]
    first_half = values[..., :half_dim]
    second = values[..., half_dim:]
    return jnp.concatenate(
        [first_half * cosine - second * sine_part, second * cosine + first_half * sine_part],
        axis=-1,
    )


def local(
    hidden,
    kv_cache,
    page_table,
    cache_lens,
    parents,
    accepted,
    attn_gain,
    w_qkv,
    qk_gain,
    w_out,
    moe_gain,
    routes,
    route_weights,
    w_gate_up,
    w_down,
):
    tok_rows, model_width = hidden.shape
    th = lax.axis_index("th")
    tl = lax.axis_index("tl")
    tc = lax.axis_index("tc")
    tp_count = lax.axis_size(TP)
    req_count = lax.axis_size("req")
    slice_width = model_width // tp_count
    slice_start = ((th * lax.axis_size("tl") + tl) * lax.axis_size("tc") + tc) * slice_width
    req_local, draft_len = parents.shape
    feat_dev = w_qkv.shape[2]
    local_heads = feat_dev // HD
    ancestry, depths = tree_masks(parents)
    positions = (cache_lens[:, None] + depths).reshape(-1)
    normed_in = rms_scale(hidden.astype(jnp.float32), attn_gain).astype(jnp.bfloat16)
    projected = jnp.einsum(
        "tw,wgf->tgf", normed_in, w_qkv, preferred_element_type=jnp.float32
    )
    query_raw = projected[:, 0]
    key_raw = projected[:, 1]
    values_new = projected[:, 2].astype(jnp.bfloat16)
    swap = [(0, 1), (1, 0)]
    squares = jnp.stack(
        [jnp.sum(query_raw * query_raw, axis=-1), jnp.sum(key_raw * key_raw, axis=-1)]
    )
    squares = squares + lax.ppermute(squares, "tc", swap)
    squares = squares + lax.ppermute(squares, "tl", swap)
    squares = squares + lax.ppermute(squares, "th", swap)
    query_normed = query_raw * lax.rsqrt(squares[0][:, None] / model_width + norm_eps) * qk_gain[0]
    key_normed = key_raw * lax.rsqrt(squares[1][:, None] / model_width + norm_eps) * qk_gain[1]
    query_rot = rotate(query_normed.reshape(tok_rows, local_heads, HD), positions).astype(
        jnp.bfloat16
    )
    keys_new = rotate(key_normed.reshape(tok_rows, local_heads, HD), positions).astype(jnp.bfloat16)
    local_pages, page_len = kv_cache.shape[1], kv_cache.shape[2]
    all_keys = kv_cache[0].reshape(local_pages * page_len, feat_dev)
    all_values = kv_cache[1].reshape(local_pages * page_len, feat_dev)
    page_ids = jnp.arange(local_pages, dtype=jnp.int32)
    page_match = (page_table[:, :, None] == page_ids[None, None, :]).astype(jnp.int32)
    page_owned = jnp.sum(page_match, axis=1)
    page_start = jnp.sum(
        page_match * (jnp.arange(page_table.shape[1], dtype=jnp.int32) * page_len)[None, :, None],
        axis=1,
    )
    key_pos = (page_start[:, :, None] + jnp.arange(page_len, dtype=jnp.int32)[None, None, :]).reshape(
        req_local, local_pages * page_len
    )
    live_keys = (jnp.repeat(page_owned, page_len, axis=1) > 0) & (key_pos < cache_lens[:, None])
    score_scale = HD ** (-0.5)
    head_outputs = []
    for head in range(local_heads):
        lanes = slice(head * HD, (head + 1) * HD)
        queries = query_rot[:, head].reshape(req_local, draft_len, HD)
        own_keys = keys_new[:, head].reshape(req_local, draft_len, HD)
        own_values = values_new[:, lanes].reshape(req_local, draft_len, HD)
        cache_scores = (
            jnp.einsum(
                "rjd,cd->rjc", queries, all_keys[:, lanes], preferred_element_type=jnp.float32
            )
            * score_scale
        )
        cache_scores = jnp.where(live_keys[:, None, :], cache_scores, masked_score)
        draft_scores = (
            jnp.einsum("rjd,rid->rji", queries, own_keys, preferred_element_type=jnp.float32)
            * score_scale
        )
        draft_scores = jnp.where(ancestry > 0.5, draft_scores, masked_score)
        row_max = jnp.maximum(
            jnp.max(cache_scores, axis=-1, keepdims=True),
            jnp.max(draft_scores, axis=-1, keepdims=True),
        )
        cache_weights = jnp.exp(cache_scores - row_max)
        draft_weights = jnp.exp(draft_scores - row_max)
        total = jnp.sum(cache_weights, axis=-1, keepdims=True) + jnp.sum(
            draft_weights, axis=-1, keepdims=True
        )
        cache_probs = (cache_weights / total).astype(jnp.bfloat16)
        draft_probs = (draft_weights / total).astype(jnp.bfloat16)
        mixed = jnp.einsum(
            "rjc,cd->rjd", cache_probs, all_values[:, lanes], preferred_element_type=jnp.float32
        ) + jnp.einsum("rji,rid->rjd", draft_probs, own_values, preferred_element_type=jnp.float32)
        head_outputs.append(mixed.astype(jnp.bfloat16).reshape(tok_rows, HD))
    attn_heads = jnp.concatenate(head_outputs, axis=1)
    attn_term = jnp.dot(attn_heads, w_out, preferred_element_type=jnp.float32)
    column_groups = model_width // (2 * slice_width)
    attn_blocks = attn_term.reshape(tok_rows, column_groups, 2, slice_width)
    kept = lax.dynamic_index_in_dim(attn_blocks, tc, axis=2, keepdims=False)
    given = lax.dynamic_index_in_dim(attn_blocks, 1 - tc, axis=2, keepdims=False)
    chip_sum = kept + lax.ppermute(given.astype(jnp.bfloat16), "tc", swap).astype(jnp.float32)
    hidden_blocks = hidden.astype(jnp.float32).reshape(tok_rows, column_groups, 2, slice_width)
    pair_blocks = chip_sum.reshape(tok_rows, column_groups // 2, 2, slice_width)
    row_sum = lax.dynamic_index_in_dim(pair_blocks, tl, axis=2, keepdims=False) + lax.ppermute(
        lax.dynamic_index_in_dim(pair_blocks, 1 - tl, axis=2, keepdims=False).astype(jnp.bfloat16),
        "tl",
        swap,
    ).astype(jnp.float32)
    block_sum = lax.dynamic_index_in_dim(row_sum, th, axis=1, keepdims=False) + lax.ppermute(
        lax.dynamic_index_in_dim(row_sum, 1 - th, axis=1, keepdims=False).astype(jnp.bfloat16),
        "th",
        swap,
    ).astype(jnp.float32)
    block_other = lax.ppermute(block_sum.astype(jnp.bfloat16), "th", swap).astype(jnp.float32)
    row_sum = jnp.where(
        th == 0,
        jnp.stack([block_sum, block_other], axis=1),
        jnp.stack([block_other, block_sum], axis=1),
    )
    row_other = lax.ppermute(row_sum.astype(jnp.bfloat16), "tl", swap).astype(jnp.float32)
    full_sum = jnp.where(
        tl == 0,
        jnp.stack([row_sum, row_other], axis=2),
        jnp.stack([row_other, row_sum], axis=2),
    ).reshape(tok_rows, column_groups, slice_width)
    residual = lax.dynamic_index_in_dim(hidden_blocks, tc, axis=2, keepdims=False) + full_sum
    own_squares = jnp.sum(residual * residual, axis=(1, 2))
    all_squares = own_squares + lax.ppermute(own_squares, "tc", swap)
    gain_here = lax.dynamic_index_in_dim(
        moe_gain.reshape(column_groups, 2, slice_width), tc, axis=1, keepdims=False
    )
    normed_half = (
        residual * lax.rsqrt(all_squares / model_width + norm_eps)[:, None, None] * gain_here
    ).astype(jnp.bfloat16).reshape(tok_rows, column_groups * slice_width)
    residual_share = lax.dynamic_index_in_dim(
        residual, th * lax.axis_size("tl") + tl, axis=1, keepdims=False
    )
    experts_here = EXPERTS // req_count
    units_dev = w_down.shape[1]
    tok_ids = jnp.arange(tok_rows, dtype=jnp.int32)
    route_hot = (routes[:, :, None] == jnp.arange(EXPERTS, dtype=jnp.int32)).astype(jnp.float32)
    per_token = jnp.sum(route_hot, axis=1)
    weight_of = jnp.sum(route_weights[:, :, None] * route_hot, axis=1)
    earlier = (tok_ids[:, None] > tok_ids[None, :]).astype(jnp.bfloat16)
    slot_of = jnp.dot(earlier, per_token.astype(jnp.bfloat16), preferred_element_type=jnp.float32)
    capacity = CAP
    cap_ids = jnp.arange(capacity, dtype=jnp.float32)
    picked_here = lax.dynamic_index_in_dim(
        per_token.reshape(tok_rows, req_count, experts_here), th, axis=2, keepdims=False
    ).T
    slot_here = lax.dynamic_index_in_dim(
        slot_of.reshape(tok_rows, req_count, experts_here), th, axis=2, keepdims=False
    ).T
    select = jnp.where(
        (picked_here[:, None, :] > 0.5) & (slot_here[:, None, :] == cap_ids[None, :, None]), 1.0, 0.0
    ).astype(jnp.bfloat16)
    send_rows = jnp.einsum(
        "ict,tw->icw", select, normed_half, preferred_element_type=jnp.float32
    ).astype(jnp.bfloat16)
    received = lax.all_to_all(send_rows, "req", 0, 0, tiled=True)
    partner_rows = lax.ppermute(received, "tc", [(0, 1), (1, 0)])
    weight_blocks = w_gate_up[0].reshape(column_groups, 2, slice_width, 2, units_dev)
    own_weights = lax.dynamic_index_in_dim(weight_blocks, tc, axis=1, keepdims=False).reshape(
        model_width // 2, 2, units_dev
    )
    partner_weights = lax.dynamic_index_in_dim(
        weight_blocks, 1 - tc, axis=1, keepdims=False
    ).reshape(model_width // 2, 2, units_dev)
    gate_up = jnp.einsum(
        "scw,wgu->scgu", received, own_weights, preferred_element_type=jnp.float32
    ) + jnp.einsum(
        "scw,wgu->scgu", partner_rows, partner_weights, preferred_element_type=jnp.float32
    )
    activated = (jax.nn.silu(gate_up[..., 0, :]) * gate_up[..., 1, :]).astype(jnp.bfloat16)
    down = (
        w_down[0]
        .reshape(units_dev, 2, 2, 2, slice_width)
        .transpose(0, 3, 2, 1, 4)
        .reshape(units_dev, model_width)
    )
    partial = jnp.einsum(
        "scu,uw->scw", activated, down, preferred_element_type=jnp.float32
    ).astype(jnp.bfloat16)
    swap = [(0, 1), (1, 0)]
    half = model_width // 2
    kept = lax.dynamic_slice_in_dim(partial, tc * half, half, 2)
    given = lax.dynamic_slice_in_dim(partial, (1 - tc) * half, half, 2)
    pair_sum = kept.astype(jnp.float32) + lax.ppermute(given, "tc", swap).astype(jnp.float32)
    quarter = half // 2
    kept = lax.dynamic_slice_in_dim(pair_sum, tl * quarter, quarter, 2)
    given = lax.dynamic_slice_in_dim(pair_sum, (1 - tl) * quarter, quarter, 2).astype(jnp.bfloat16)
    quad_sum = (kept + lax.ppermute(given, "tl", swap).astype(jnp.float32)).astype(jnp.bfloat16)
    back = (
        quad_sum.reshape(req_count, capacity, 2, slice_width)
        .transpose(0, 2, 1, 3)
        .reshape(req_count * 2, capacity, slice_width)
    )
    returned = lax.all_to_all(back, ("req", "th"), 0, 0, tiled=True)
    combine = weight_of[:, :, None] * (slot_of[:, :, None] == cap_ids[None, None, :])
    mixture = jnp.dot(
        combine.reshape(tok_rows, EXPERTS * capacity),
        returned.reshape(EXPERTS * capacity, slice_width).astype(jnp.float32),
        precision=lax.Precision.HIGHEST,
        preferred_element_type=jnp.float32,
    )
    output = (residual_share + mixture).astype(jnp.bfloat16)
    picked_rows = (jnp.arange(req_local, dtype=jnp.int32)[:, None] * draft_len + accepted).reshape(
        -1
    )
    accepted_kv = jnp.stack(
        [keys_new.reshape(tok_rows, feat_dev)[picked_rows], values_new[picked_rows]]
    )
    return (output, accepted_kv)


def solution(mesh):
    req_count = mesh.shape["req"]
    devices = mesh.devices.reshape(req_count, 2, 2, mesh.shape["tp"] // 4)
    split_mesh = Mesh(devices, ("req",) + TP)
    return jax.shard_map(
        local,
        mesh=split_mesh,
        in_specs=(
            P("req", None),
            P(None, "req", None, TP),
            P("req", None),
            P("req"),
            P("req", None),
            P("req", None),
            P(),
            P(None, None, TP),
            P(None, TP),
            P(TP, None),
            P(),
            P("req", None),
            P("req", None),
            P("req", None, None, TP),
            P("req", TP, None),
        ),
        out_specs=(P("req", TP), P(None, "req", TP)),
        check_vma=False,
    )
```

```python
import jax
import jax.numpy as jnp
from jax import lax
from jax.sharding import Mesh, PartitionSpec as P

HD = 128
FFE = 1024
EXPERTS = 64
CAP = 40
TP = ("th", "tl", "tc")


norm_eps = 1e-05
rope_base = 10000.0
masked_score = -1e30


def rms_scale(values, gain):
    return values * lax.rsqrt(jnp.mean(values * values, axis=-1, keepdims=True) + norm_eps) * gain


def tree_masks(parents):
    slot_count = parents.shape[-1]
    slot_ids = jnp.arange(slot_count, dtype=jnp.int32)
    parent_hot = (parents[..., :, None] == slot_ids).astype(jnp.float32)
    ancestry = jnp.minimum(jnp.eye(slot_count, dtype=jnp.float32) + parent_hot, 1.0)
    for squaring in range(slot_count.bit_length()):
        ancestry = jnp.minimum(
            jnp.einsum("rij,rjk->rik", ancestry, ancestry, precision=lax.Precision.HIGHEST), 1.0
        )
    depths = jnp.sum(ancestry, axis=-1).astype(jnp.int32) - 1
    return (ancestry, depths)


def rotate(values, positions):
    head_dim = values.shape[-1]
    half_dim = head_dim // 2
    frequency = rope_base ** (-jnp.arange(half_dim, dtype=jnp.float32) * 2.0 / head_dim)
    angles = positions.astype(jnp.float32)[:, None] * frequency[None, :]
    cosine = jnp.cos(angles)[:, None, :]
    sine_part = jnp.sin(angles)[:, None, :]
    first_half = values[..., :half_dim]
    second = values[..., half_dim:]
    return jnp.concatenate(
        [first_half * cosine - second * sine_part, second * cosine + first_half * sine_part],
        axis=-1,
    )


def local(
    hidden,
    kv_cache,
    page_table,
    cache_lens,
    parents,
    accepted,
    attn_gain,
    w_qkv,
    qk_gain,
    w_out,
    moe_gain,
    routes,
    route_weights,
    w_gate_up,
    w_down,
):
    tok_rows, model_width = hidden.shape
    th = lax.axis_index("th")
    tl = lax.axis_index("tl")
    tc = lax.axis_index("tc")
    tp_count = lax.axis_size(TP)
    req_count = lax.axis_size("req")
    slice_width = model_width // tp_count
    slice_start = ((th * lax.axis_size("tl") + tl) * lax.axis_size("tc") + tc) * slice_width
    req_local, draft_len = parents.shape
    feat_dev = w_qkv.shape[2]
    local_heads = feat_dev // HD
    ancestry, depths = tree_masks(parents)
    positions = (cache_lens[:, None] + depths).reshape(-1)
    normed_in = rms_scale(hidden.astype(jnp.float32), attn_gain).astype(jnp.bfloat16)
    projected = jnp.einsum(
        "tw,wgf->tgf", normed_in, w_qkv, preferred_element_type=jnp.float32
    )
    query_raw = projected[:, 0]
    key_raw = projected[:, 1]
    values_new = projected[:, 2].astype(jnp.bfloat16)
    swap = [(0, 1), (1, 0)]
    squares = jnp.stack(
        [jnp.sum(query_raw * query_raw, axis=-1), jnp.sum(key_raw * key_raw, axis=-1)]
    )
    tp_ring = [[(src, (src + shift) % tp_count) for src in range(tp_count)] for shift in range(1, tp_count)]
    squares = squares + sum(lax.ppermute(squares, TP, ring) for ring in tp_ring)
    query_normed = query_raw * lax.rsqrt(squares[0][:, None] / model_width + norm_eps) * qk_gain[0]
    key_normed = key_raw * lax.rsqrt(squares[1][:, None] / model_width + norm_eps) * qk_gain[1]
    query_rot = rotate(query_normed.reshape(tok_rows, local_heads, HD), positions).astype(
        jnp.bfloat16
    )
    keys_new = rotate(key_normed.reshape(tok_rows, local_heads, HD), positions).astype(jnp.bfloat16)
    local_pages, page_len = kv_cache.shape[1], kv_cache.shape[2]
    all_keys = kv_cache[0].reshape(local_pages * page_len, feat_dev)
    all_values = kv_cache[1].reshape(local_pages * page_len, feat_dev)
    page_ids = jnp.arange(local_pages, dtype=jnp.int32)
    page_match = (page_table[:, :, None] == page_ids[None, None, :]).astype(jnp.int32)
    page_owned = jnp.sum(page_match, axis=1)
    page_start = jnp.sum(
        page_match * (jnp.arange(page_table.shape[1], dtype=jnp.int32) * page_len)[None, :, None],
        axis=1,
    )
    key_pos = (page_start[:, :, None] + jnp.arange(page_len, dtype=jnp.int32)[None, None, :]).reshape(
        req_local, local_pages * page_len
    )
    live_keys = (jnp.repeat(page_owned, page_len, axis=1) > 0) & (key_pos < cache_lens[:, None])
    score_scale = HD ** (-0.5)
    head_outputs = []
    for head in range(local_heads):
        lanes = slice(head * HD, (head + 1) * HD)
        queries = query_rot[:, head].reshape(req_local, draft_len, HD)
        own_keys = keys_new[:, head].reshape(req_local, draft_len, HD)
        own_values = values_new[:, lanes].reshape(req_local, draft_len, HD)
        cache_scores = (
            jnp.einsum(
                "rjd,cd->rjc", queries, all_keys[:, lanes], preferred_element_type=jnp.float32
            )
            * score_scale
        )
        cache_scores = jnp.where(live_keys[:, None, :], cache_scores, masked_score)
        draft_scores = (
            jnp.einsum("rjd,rid->rji", queries, own_keys, preferred_element_type=jnp.float32)
            * score_scale
        )
        draft_scores = jnp.where(ancestry > 0.5, draft_scores, masked_score)
        row_max = jnp.maximum(
            jnp.max(cache_scores, axis=-1, keepdims=True),
            jnp.max(draft_scores, axis=-1, keepdims=True),
        )
        cache_weights = jnp.exp(cache_scores - row_max)
        draft_weights = jnp.exp(draft_scores - row_max)
        total = jnp.sum(cache_weights, axis=-1, keepdims=True) + jnp.sum(
            draft_weights, axis=-1, keepdims=True
        )
        cache_probs = (cache_weights / total).astype(jnp.bfloat16)
        draft_probs = (draft_weights / total).astype(jnp.bfloat16)
        mixed = jnp.einsum(
            "rjc,cd->rjd", cache_probs, all_values[:, lanes], preferred_element_type=jnp.float32
        ) + jnp.einsum("rji,rid->rjd", draft_probs, own_values, preferred_element_type=jnp.float32)
        head_outputs.append(mixed.astype(jnp.bfloat16).reshape(tok_rows, HD))
    attn_heads = jnp.concatenate(head_outputs, axis=1)
    attn_term = jnp.dot(attn_heads, w_out, preferred_element_type=jnp.float32)
    column_groups = model_width // (2 * slice_width)
    attn_blocks = attn_term.reshape(tok_rows, column_groups, 2, slice_width)
    kept = lax.dynamic_index_in_dim(attn_blocks, tc, axis=2, keepdims=False)
    given = lax.dynamic_index_in_dim(attn_blocks, 1 - tc, axis=2, keepdims=False)
    chip_sum = kept + lax.ppermute(given.astype(jnp.bfloat16), "tc", swap).astype(jnp.float32)
    hidden_blocks = hidden.astype(jnp.float32).reshape(tok_rows, column_groups, 2, slice_width)
    chip_axes = ("th", "tl")
    chip_index = th * lax.axis_size("tl") + tl
    chips = column_groups
    shifts = range(1, chips)
    block_sum = lax.dynamic_index_in_dim(chip_sum, chip_index, axis=1, keepdims=False)
    for shift in shifts:
        outgoing = lax.dynamic_index_in_dim(
            chip_sum, (chip_index + shift) % chips, axis=1, keepdims=False
        ).astype(jnp.bfloat16)
        ring = [(src, (src + shift) % chips) for src in range(chips)]
        block_sum = block_sum + lax.ppermute(outgoing, chip_axes, ring).astype(jnp.float32)
    shared = block_sum.astype(jnp.bfloat16)
    gathered = jnp.stack(
        [block_sum]
        + [
            lax.ppermute(shared, chip_axes, [(src, (src + shift) % chips) for src in range(chips)]).astype(
                jnp.float32
            )
            for shift in shifts
        ]
    )
    order = (chip_index - jnp.arange(chips, dtype=jnp.int32)) % chips
    full_sum = jnp.take(gathered, order, axis=0).transpose(1, 0, 2)
    residual = lax.dynamic_index_in_dim(hidden_blocks, tc, axis=2, keepdims=False) + full_sum
    own_squares = jnp.sum(residual * residual, axis=(1, 2))
    all_squares = own_squares + lax.ppermute(own_squares, "tc", swap)
    gain_here = lax.dynamic_index_in_dim(
        moe_gain.reshape(column_groups, 2, slice_width), tc, axis=1, keepdims=False
    )
    normed_half = (
        residual * lax.rsqrt(all_squares / model_width + norm_eps)[:, None, None] * gain_here
    ).astype(jnp.bfloat16).reshape(tok_rows, column_groups * slice_width)
    residual_share = lax.dynamic_index_in_dim(
        residual, th * lax.axis_size("tl") + tl, axis=1, keepdims=False
    )
    experts_here = EXPERTS // req_count
    units_dev = w_down.shape[1]
    tok_ids = jnp.arange(tok_rows, dtype=jnp.int32)
    route_hot = (routes[:, :, None] == jnp.arange(EXPERTS, dtype=jnp.int32)).astype(jnp.float32)
    per_token = jnp.sum(route_hot, axis=1)
    weight_of = jnp.sum(route_weights[:, :, None] * route_hot, axis=1)
    earlier = (tok_ids[:, None] > tok_ids[None, :]).astype(jnp.bfloat16)
    slot_of = jnp.dot(earlier, per_token.astype(jnp.bfloat16), preferred_element_type=jnp.float32)
    capacity = CAP
    cap_ids = jnp.arange(capacity, dtype=jnp.float32)
    picked_here = lax.dynamic_index_in_dim(
        per_token.reshape(tok_rows, req_count, experts_here), th, axis=2, keepdims=False
    ).T
    slot_here = lax.dynamic_index_in_dim(
        slot_of.reshape(tok_rows, req_count, experts_here), th, axis=2, keepdims=False
    ).T
    select = jnp.where(
        (picked_here[:, None, :] > 0.5) & (slot_here[:, None, :] == cap_ids[None, :, None]), 1.0, 0.0
    ).astype(jnp.bfloat16)
    send_rows = jnp.einsum(
        "ict,tw->icw", select, normed_half, preferred_element_type=jnp.float32
    ).astype(jnp.bfloat16)
    received = lax.all_to_all(send_rows, "req", 0, 0, tiled=True)
    partner_rows = lax.ppermute(received, "tc", [(0, 1), (1, 0)])
    weight_blocks = w_gate_up[0].reshape(column_groups, 2, slice_width, 2, units_dev)
    own_weights = lax.dynamic_index_in_dim(weight_blocks, tc, axis=1, keepdims=False).reshape(
        model_width // 2, 2, units_dev
    )
    partner_weights = lax.dynamic_index_in_dim(
        weight_blocks, 1 - tc, axis=1, keepdims=False
    ).reshape(model_width // 2, 2, units_dev)
    gate_up = jnp.einsum(
        "scw,wgu->scgu", received, own_weights, preferred_element_type=jnp.float32
    ) + jnp.einsum(
        "scw,wgu->scgu", partner_rows, partner_weights, preferred_element_type=jnp.float32
    )
    activated = (jax.nn.silu(gate_up[..., 0, :]) * gate_up[..., 1, :]).astype(jnp.bfloat16)
    down = (
        w_down[0]
        .reshape(units_dev, 2, 2, 2, slice_width)
        .transpose(0, 3, 2, 1, 4)
        .reshape(units_dev, model_width)
    )
    partial = jnp.einsum(
        "scu,uw->scw", activated, down, preferred_element_type=jnp.float32
    ).astype(jnp.bfloat16)
    swap = [(0, 1), (1, 0)]
    half = model_width // 2
    kept = lax.dynamic_slice_in_dim(partial, tc * half, half, 2)
    given = lax.dynamic_slice_in_dim(partial, (1 - tc) * half, half, 2)
    pair_sum = kept.astype(jnp.float32) + lax.ppermute(given, "tc", swap).astype(jnp.float32)
    quarter = half // 2
    kept = lax.dynamic_slice_in_dim(pair_sum, tl * quarter, quarter, 2)
    given = lax.dynamic_slice_in_dim(pair_sum, (1 - tl) * quarter, quarter, 2).astype(jnp.bfloat16)
    quad_sum = (kept + lax.ppermute(given, "tl", swap).astype(jnp.float32)).astype(jnp.bfloat16)
    back = (
        quad_sum.reshape(req_count, capacity, 2, slice_width)
        .transpose(0, 2, 1, 3)
        .reshape(req_count * 2, capacity, slice_width)
    )
    returned = lax.all_to_all(back, ("req", "th"), 0, 0, tiled=True)
    combine = weight_of[:, :, None] * (slot_of[:, :, None] == cap_ids[None, None, :])
    mixture = jnp.dot(
        combine.reshape(tok_rows, EXPERTS * capacity),
        returned.reshape(EXPERTS * capacity, slice_width).astype(jnp.float32),
        precision=lax.Precision.HIGHEST,
        preferred_element_type=jnp.float32,
    )
    output = (residual_share + mixture).astype(jnp.bfloat16)
    picked_rows = (jnp.arange(req_local, dtype=jnp.int32)[:, None] * draft_len + accepted).reshape(
        -1
    )
    accepted_kv = jnp.stack(
        [keys_new.reshape(tok_rows, feat_dev)[picked_rows], values_new[picked_rows]]
    )
    return (output, accepted_kv)


def solution(mesh):
    req_count = mesh.shape["req"]
    devices = mesh.devices.reshape(req_count, 2, 2, mesh.shape["tp"] // 4)
    split_mesh = Mesh(devices, ("req",) + TP)
    return jax.shard_map(
        local,
        mesh=split_mesh,
        in_specs=(
            P("req", None),
            P(None, "req", None, TP),
            P("req", None),
            P("req"),
            P("req", None),
            P("req", None),
            P(),
            P(None, None, TP),
            P(None, TP),
            P(TP, None),
            P(),
            P("req", None),
            P("req", None),
            P("req", None, None, TP),
            P("req", TP, None),
        ),
        out_specs=(P("req", TP), P(None, "req", TP)),
        check_vma=False,
    )
```

```python
import jax
import jax.numpy as jnp
from jax import lax
from jax.sharding import Mesh, PartitionSpec as P

HD = 128
FFE = 1024
EXPERTS = 64
CAP = 40
TP = ("th", "tl", "tc")


norm_eps = 1e-05
rope_base = 10000.0
masked_score = -1e30


def rms_scale(values, gain):
    return values * lax.rsqrt(jnp.mean(values * values, axis=-1, keepdims=True) + norm_eps) * gain


def tree_masks(parents):
    slot_count = parents.shape[-1]
    slot_ids = jnp.arange(slot_count, dtype=jnp.int32)
    parent_hot = (parents[..., :, None] == slot_ids).astype(jnp.float32)
    ancestry = jnp.minimum(jnp.eye(slot_count, dtype=jnp.float32) + parent_hot, 1.0)
    for squaring in range(slot_count.bit_length()):
        ancestry = jnp.minimum(
            jnp.einsum("rij,rjk->rik", ancestry, ancestry, precision=lax.Precision.HIGHEST), 1.0
        )
    depths = jnp.sum(ancestry, axis=-1).astype(jnp.int32) - 1
    return (ancestry, depths)


def rotate(values, positions):
    head_dim = values.shape[-1]
    half_dim = head_dim // 2
    frequency = rope_base ** (-jnp.arange(half_dim, dtype=jnp.float32) * 2.0 / head_dim)
    angles = positions.astype(jnp.float32)[:, None] * frequency[None, :]
    cosine = jnp.cos(angles)[:, None, :]
    sine_part = jnp.sin(angles)[:, None, :]
    first_half = values[..., :half_dim]
    second = values[..., half_dim:]
    return jnp.concatenate(
        [first_half * cosine - second * sine_part, second * cosine + first_half * sine_part],
        axis=-1,
    )


def local(
    hidden,
    kv_cache,
    page_table,
    cache_lens,
    parents,
    accepted,
    attn_gain,
    w_qkv,
    qk_gain,
    w_out,
    moe_gain,
    routes,
    route_weights,
    w_gate_up,
    w_down,
):
    tok_rows, model_width = hidden.shape
    th = lax.axis_index("th")
    tl = lax.axis_index("tl")
    tc = lax.axis_index("tc")
    tp_count = lax.axis_size(TP)
    req_count = lax.axis_size("req")
    slice_width = model_width // tp_count
    slice_start = ((th * lax.axis_size("tl") + tl) * lax.axis_size("tc") + tc) * slice_width
    req_local, draft_len = parents.shape
    feat_dev = w_qkv.shape[2]
    local_heads = feat_dev // HD
    ancestry, depths = tree_masks(parents)
    positions = (cache_lens[:, None] + depths).reshape(-1)
    normed_in = rms_scale(hidden.astype(jnp.float32), attn_gain).astype(jnp.bfloat16)
    projected = jnp.einsum(
        "tw,wgf->tgf", normed_in, w_qkv, preferred_element_type=jnp.float32
    )
    query_raw = projected[:, 0]
    key_raw = projected[:, 1]
    values_new = projected[:, 2].astype(jnp.bfloat16)
    swap = [(0, 1), (1, 0)]
    squares = jnp.stack(
        [jnp.sum(query_raw * query_raw, axis=-1), jnp.sum(key_raw * key_raw, axis=-1)]
    )
    tp_ring = [[(src, (src + shift) % tp_count) for src in range(tp_count)] for shift in range(1, tp_count)]
    squares = squares + sum(lax.ppermute(squares, TP, ring) for ring in tp_ring)
    query_normed = query_raw * lax.rsqrt(squares[0][:, None] / model_width + norm_eps) * qk_gain[0]
    key_normed = key_raw * lax.rsqrt(squares[1][:, None] / model_width + norm_eps) * qk_gain[1]
    query_rot = rotate(query_normed.reshape(tok_rows, local_heads, HD), positions).astype(
        jnp.bfloat16
    )
    keys_new = rotate(key_normed.reshape(tok_rows, local_heads, HD), positions).astype(jnp.bfloat16)
    local_pages, page_len = kv_cache.shape[1], kv_cache.shape[2]
    all_keys = kv_cache[0].reshape(local_pages * page_len, feat_dev)
    all_values = kv_cache[1].reshape(local_pages * page_len, feat_dev)
    page_ids = jnp.arange(local_pages, dtype=jnp.int32)
    page_match = (page_table[:, :, None] == page_ids[None, None, :]).astype(jnp.int32)
    page_owned = jnp.sum(page_match, axis=1)
    page_start = jnp.sum(
        page_match * (jnp.arange(page_table.shape[1], dtype=jnp.int32) * page_len)[None, :, None],
        axis=1,
    )
    key_pos = (page_start[:, :, None] + jnp.arange(page_len, dtype=jnp.int32)[None, None, :]).reshape(
        req_local, local_pages * page_len
    )
    live_keys = (jnp.repeat(page_owned, page_len, axis=1) > 0) & (key_pos < cache_lens[:, None])
    score_scale = HD ** (-0.5)
    head_outputs = []
    for head in range(local_heads):
        lanes = slice(head * HD, (head + 1) * HD)
        queries = query_rot[:, head].reshape(req_local, draft_len, HD)
        own_keys = keys_new[:, head].reshape(req_local, draft_len, HD)
        own_values = values_new[:, lanes].reshape(req_local, draft_len, HD)
        cache_scores = (
            jnp.einsum(
                "rjd,cd->rjc", queries, all_keys[:, lanes], preferred_element_type=jnp.float32
            )
            * score_scale
        )
        cache_scores = jnp.where(live_keys[:, None, :], cache_scores, masked_score)
        draft_scores = (
            jnp.einsum("rjd,rid->rji", queries, own_keys, preferred_element_type=jnp.float32)
            * score_scale
        )
        draft_scores = jnp.where(ancestry > 0.5, draft_scores, masked_score)
        row_max = jnp.maximum(
            jnp.max(cache_scores, axis=-1, keepdims=True),
            jnp.max(draft_scores, axis=-1, keepdims=True),
        )
        cache_weights = jnp.exp(cache_scores - row_max)
        draft_weights = jnp.exp(draft_scores - row_max)
        total = jnp.sum(cache_weights, axis=-1, keepdims=True) + jnp.sum(
            draft_weights, axis=-1, keepdims=True
        )
        cache_probs = (cache_weights / total).astype(jnp.bfloat16)
        draft_probs = (draft_weights / total).astype(jnp.bfloat16)
        mixed = jnp.einsum(
            "rjc,cd->rjd", cache_probs, all_values[:, lanes], preferred_element_type=jnp.float32
        ) + jnp.einsum("rji,rid->rjd", draft_probs, own_values, preferred_element_type=jnp.float32)
        head_outputs.append(mixed.astype(jnp.bfloat16).reshape(tok_rows, HD))
    attn_heads = jnp.concatenate(head_outputs, axis=1)
    attn_term = jnp.dot(attn_heads, w_out, preferred_element_type=jnp.float32)
    column_groups = model_width // (2 * slice_width)
    attn_blocks = attn_term.reshape(tok_rows, column_groups, 2, slice_width)
    kept = lax.dynamic_index_in_dim(attn_blocks, tc, axis=2, keepdims=False)
    given = lax.dynamic_index_in_dim(attn_blocks, 1 - tc, axis=2, keepdims=False)
    chip_sum = kept + lax.ppermute(given.astype(jnp.bfloat16), "tc", swap).astype(jnp.float32)
    hidden_blocks = hidden.astype(jnp.float32).reshape(tok_rows, column_groups, 2, slice_width)
    chip_axes = ("th", "tl")
    chip_index = th * lax.axis_size("tl") + tl
    chips = column_groups
    shifts = range(1, chips)
    block_sum = lax.dynamic_index_in_dim(chip_sum, chip_index, axis=1, keepdims=False)
    for shift in shifts:
        outgoing = lax.dynamic_index_in_dim(
            chip_sum, (chip_index + shift) % chips, axis=1, keepdims=False
        ).astype(jnp.bfloat16)
        ring = [(src, (src + shift) % chips) for src in range(chips)]
        block_sum = block_sum + lax.ppermute(outgoing, chip_axes, ring).astype(jnp.float32)
    shared = block_sum.astype(jnp.bfloat16)
    gathered = jnp.stack(
        [block_sum]
        + [
            lax.ppermute(shared, chip_axes, [(src, (src + shift) % chips) for src in range(chips)]).astype(
                jnp.float32
            )
            for shift in shifts
        ]
    )
    order = (chip_index - jnp.arange(chips, dtype=jnp.int32)) % chips
    full_sum = jnp.take(gathered, order, axis=0).transpose(1, 0, 2)
    residual = lax.dynamic_index_in_dim(hidden_blocks, tc, axis=2, keepdims=False) + full_sum
    own_squares = jnp.sum(residual * residual, axis=(1, 2))
    all_squares = own_squares + lax.ppermute(own_squares, "tc", swap)
    gain_here = lax.dynamic_index_in_dim(
        moe_gain.reshape(column_groups, 2, slice_width), tc, axis=1, keepdims=False
    )
    normed_half = (
        residual * lax.rsqrt(all_squares / model_width + norm_eps)[:, None, None] * gain_here
    ).astype(jnp.bfloat16).reshape(tok_rows, column_groups * slice_width)
    residual_share = lax.dynamic_index_in_dim(
        residual, th * lax.axis_size("tl") + tl, axis=1, keepdims=False
    )
    experts_here = EXPERTS // req_count
    units_dev = w_down.shape[1]
    tok_ids = jnp.arange(tok_rows, dtype=jnp.int32)
    route_hot = (routes[:, :, None] == jnp.arange(EXPERTS, dtype=jnp.int32)).astype(jnp.float32)
    per_token = jnp.sum(route_hot, axis=1)
    weight_of = jnp.sum(route_weights[:, :, None] * route_hot, axis=1)
    earlier = (tok_ids[:, None] > tok_ids[None, :]).astype(jnp.bfloat16)
    slot_of = jnp.dot(earlier, per_token.astype(jnp.bfloat16), preferred_element_type=jnp.float32)
    capacity = CAP
    cap_ids = jnp.arange(capacity, dtype=jnp.float32)
    picked_here = lax.dynamic_index_in_dim(
        per_token.reshape(tok_rows, req_count, experts_here), th, axis=2, keepdims=False
    ).T
    slot_here = lax.dynamic_index_in_dim(
        slot_of.reshape(tok_rows, req_count, experts_here), th, axis=2, keepdims=False
    ).T
    select = jnp.where(
        (picked_here[:, None, :] > 0.5) & (slot_here[:, None, :] == cap_ids[None, :, None]), 1.0, 0.0
    ).astype(jnp.bfloat16)
    normed_quarter = lax.dynamic_index_in_dim(
        normed_half.reshape(tok_rows, 2, 2, slice_width), tl, axis=2, keepdims=False
    ).reshape(tok_rows, 2 * slice_width)
    send_rows = jnp.einsum(
        "ict,tw->icw", select, normed_quarter, preferred_element_type=jnp.float32
    ).astype(jnp.bfloat16)
    received = lax.all_to_all(send_rows, "req", 0, 0, tiled=True)
    from_core = lax.ppermute(received, "tc", swap)
    from_chip = lax.ppermute(received, "tl", swap)
    from_diagonal = lax.ppermute(from_chip, "tc", swap)
    weight_blocks = w_gate_up[0].reshape(2, 2, 2, slice_width, 2, units_dev)

    def quarter_weights(chip_half, core_half):
        picked = lax.dynamic_index_in_dim(weight_blocks, chip_half, axis=1, keepdims=False)
        picked = lax.dynamic_index_in_dim(picked, core_half, axis=1, keepdims=False)
        return picked.reshape(2 * slice_width, 2, units_dev)

    gate_up = None
    for rows_in, chip_half, core_half in (
        (received, tl, tc),
        (from_core, tl, 1 - tc),
        (from_chip, 1 - tl, tc),
        (from_diagonal, 1 - tl, 1 - tc),
    ):
        term = jnp.einsum(
            "scw,wgu->scgu",
            rows_in,
            quarter_weights(chip_half, core_half),
            preferred_element_type=jnp.float32,
        )
        gate_up = term if gate_up is None else gate_up + term
    activated = (jax.nn.silu(gate_up[..., 0, :]) * gate_up[..., 1, :]).astype(jnp.bfloat16)
    down = (
        w_down[0]
        .reshape(units_dev, 2, 2, 2, slice_width)
        .transpose(0, 3, 2, 1, 4)
        .reshape(units_dev, model_width)
    )
    partial = jnp.einsum(
        "scu,uw->scw", activated, down, preferred_element_type=jnp.float32
    ).astype(jnp.bfloat16)
    swap = [(0, 1), (1, 0)]
    half = model_width // 2
    kept = lax.dynamic_slice_in_dim(partial, tc * half, half, 2)
    given = lax.dynamic_slice_in_dim(partial, (1 - tc) * half, half, 2)
    pair_sum = kept.astype(jnp.float32) + lax.ppermute(given, "tc", swap).astype(jnp.float32)
    quarter = half // 2
    kept = lax.dynamic_slice_in_dim(pair_sum, tl * quarter, quarter, 2)
    given = lax.dynamic_slice_in_dim(pair_sum, (1 - tl) * quarter, quarter, 2).astype(jnp.bfloat16)
    quad_sum = (kept + lax.ppermute(given, "tl", swap).astype(jnp.float32)).astype(jnp.bfloat16)
    back = (
        quad_sum.reshape(req_count, capacity, 2, slice_width)
        .transpose(0, 2, 1, 3)
        .reshape(req_count * 2, capacity, slice_width)
    )
    returned = lax.all_to_all(back, ("req", "th"), 0, 0, tiled=True)
    combine = weight_of[:, :, None] * (slot_of[:, :, None] == cap_ids[None, None, :])
    mixture = jnp.dot(
        combine.reshape(tok_rows, EXPERTS * capacity),
        returned.reshape(EXPERTS * capacity, slice_width).astype(jnp.float32),
        precision=lax.Precision.HIGHEST,
        preferred_element_type=jnp.float32,
    )
    output = (residual_share + mixture).astype(jnp.bfloat16)
    picked_rows = (jnp.arange(req_local, dtype=jnp.int32)[:, None] * draft_len + accepted).reshape(
        -1
    )
    accepted_kv = jnp.stack(
        [keys_new.reshape(tok_rows, feat_dev)[picked_rows], values_new[picked_rows]]
    )
    return (output, accepted_kv)


def solution(mesh):
    req_count = mesh.shape["req"]
    devices = mesh.devices.reshape(req_count, 2, 2, mesh.shape["tp"] // 4)
    split_mesh = Mesh(devices, ("req",) + TP)
    return jax.shard_map(
        local,
        mesh=split_mesh,
        in_specs=(
            P("req", None),
            P(None, "req", None, TP),
            P("req", None),
            P("req"),
            P("req", None),
            P("req", None),
            P(),
            P(None, None, TP),
            P(None, TP),
            P(TP, None),
            P(),
            P("req", None),
            P("req", None),
            P("req", None, None, TP),
            P("req", TP, None),
        ),
        out_specs=(P("req", TP), P(None, "req", TP)),
        check_vma=False,
    )
```

```python
import jax
import jax.numpy as jnp
from jax import lax
from jax.sharding import Mesh, PartitionSpec as P

HD = 128
FFE = 1024
EXPERTS = 64
CAP = 40
TP = ("th", "tl", "tc")


norm_eps = 1e-05
rope_base = 10000.0
masked_score = -1e30


def rms_scale(values, gain):
    return values * lax.rsqrt(jnp.mean(values * values, axis=-1, keepdims=True) + norm_eps) * gain


def tree_masks(parents):
    slot_count = parents.shape[-1]
    slot_ids = jnp.arange(slot_count, dtype=jnp.int32)
    parent_hot = (parents[..., :, None] == slot_ids).astype(jnp.float32)
    ancestry = jnp.minimum(jnp.eye(slot_count, dtype=jnp.float32) + parent_hot, 1.0)
    for squaring in range(slot_count.bit_length()):
        hops = ancestry.astype(jnp.bfloat16)
        ancestry = jnp.minimum(
            jnp.einsum("rij,rjk->rik", hops, hops, preferred_element_type=jnp.float32), 1.0
        )
    depths = jnp.sum(ancestry, axis=-1).astype(jnp.int32) - 1
    return (ancestry, depths)


def rotate(values, positions):
    head_dim = values.shape[-1]
    half_dim = head_dim // 2
    frequency = rope_base ** (-jnp.arange(half_dim, dtype=jnp.float32) * 2.0 / head_dim)
    angles = positions.astype(jnp.float32)[:, None] * frequency[None, :]
    cosine = jnp.cos(angles)[:, None, :]
    sine_part = jnp.sin(angles)[:, None, :]
    first_half = values[..., :half_dim]
    second = values[..., half_dim:]
    return jnp.concatenate(
        [first_half * cosine - second * sine_part, second * cosine + first_half * sine_part],
        axis=-1,
    )


def local(
    hidden,
    kv_cache,
    page_table,
    cache_lens,
    parents,
    accepted,
    attn_gain,
    w_qkv,
    qk_gain,
    w_out,
    moe_gain,
    routes,
    route_weights,
    w_gate_up,
    w_down,
):
    tok_rows, model_width = hidden.shape
    th = lax.axis_index("th")
    tl = lax.axis_index("tl")
    tc = lax.axis_index("tc")
    tp_count = lax.axis_size(TP)
    req_count = lax.axis_size("req")
    slice_width = model_width // tp_count
    slice_start = ((th * lax.axis_size("tl") + tl) * lax.axis_size("tc") + tc) * slice_width
    req_local, draft_len = parents.shape
    feat_dev = w_qkv.shape[2]
    local_heads = feat_dev // HD
    ancestry, depths = tree_masks(parents)
    positions = (cache_lens[:, None] + depths).reshape(-1)
    normed_in = rms_scale(hidden.astype(jnp.float32), attn_gain).astype(jnp.bfloat16)
    projected = jnp.einsum(
        "tw,wgf->tgf", normed_in, w_qkv, preferred_element_type=jnp.float32
    )
    query_raw = projected[:, 0]
    key_raw = projected[:, 1]
    values_new = projected[:, 2].astype(jnp.bfloat16)
    swap = [(0, 1), (1, 0)]
    squares = jnp.stack(
        [jnp.sum(query_raw * query_raw, axis=-1), jnp.sum(key_raw * key_raw, axis=-1)]
    )
    tp_ring = [[(src, (src + shift) % tp_count) for src in range(tp_count)] for shift in range(1, tp_count)]
    squares = squares + sum(lax.ppermute(squares, TP, ring) for ring in tp_ring)
    query_normed = query_raw * lax.rsqrt(squares[0][:, None] / model_width + norm_eps) * qk_gain[0]
    key_normed = key_raw * lax.rsqrt(squares[1][:, None] / model_width + norm_eps) * qk_gain[1]
    query_rot = rotate(query_normed.reshape(tok_rows, local_heads, HD), positions).astype(
        jnp.bfloat16
    )
    keys_new = rotate(key_normed.reshape(tok_rows, local_heads, HD), positions).astype(jnp.bfloat16)
    local_pages, page_len = kv_cache.shape[1], kv_cache.shape[2]
    all_keys = kv_cache[0].reshape(local_pages * page_len, feat_dev)
    all_values = kv_cache[1].reshape(local_pages * page_len, feat_dev)
    page_ids = jnp.arange(local_pages, dtype=jnp.int32)
    page_match = (page_table[:, :, None] == page_ids[None, None, :]).astype(jnp.int32)
    page_owned = jnp.sum(page_match, axis=1)
    page_start = jnp.sum(
        page_match * (jnp.arange(page_table.shape[1], dtype=jnp.int32) * page_len)[None, :, None],
        axis=1,
    )
    key_pos = (page_start[:, :, None] + jnp.arange(page_len, dtype=jnp.int32)[None, None, :]).reshape(
        req_local, local_pages * page_len
    )
    live_keys = (jnp.repeat(page_owned, page_len, axis=1) > 0) & (key_pos < cache_lens[:, None])
    score_scale = HD ** (-0.5)
    head_outputs = []
    for head in range(local_heads):
        lanes = slice(head * HD, (head + 1) * HD)
        queries = query_rot[:, head].reshape(req_local, draft_len, HD)
        own_keys = keys_new[:, head].reshape(req_local, draft_len, HD)
        own_values = values_new[:, lanes].reshape(req_local, draft_len, HD)
        cache_scores = (
            jnp.einsum(
                "rjd,cd->rjc", queries, all_keys[:, lanes], preferred_element_type=jnp.float32
            )
            * score_scale
        )
        cache_scores = jnp.where(live_keys[:, None, :], cache_scores, masked_score)
        draft_scores = (
            jnp.einsum("rjd,rid->rji", queries, own_keys, preferred_element_type=jnp.float32)
            * score_scale
        )
        draft_scores = jnp.where(ancestry > 0.5, draft_scores, masked_score)
        row_max = jnp.maximum(
            jnp.max(cache_scores, axis=-1, keepdims=True),
            jnp.max(draft_scores, axis=-1, keepdims=True),
        )
        cache_weights = jnp.exp(cache_scores - row_max)
        draft_weights = jnp.exp(draft_scores - row_max)
        total = jnp.sum(cache_weights, axis=-1, keepdims=True) + jnp.sum(
            draft_weights, axis=-1, keepdims=True
        )
        cache_probs = (cache_weights / total).astype(jnp.bfloat16)
        draft_probs = (draft_weights / total).astype(jnp.bfloat16)
        mixed = jnp.einsum(
            "rjc,cd->rjd", cache_probs, all_values[:, lanes], preferred_element_type=jnp.float32
        ) + jnp.einsum("rji,rid->rjd", draft_probs, own_values, preferred_element_type=jnp.float32)
        head_outputs.append(mixed.astype(jnp.bfloat16).reshape(tok_rows, HD))
    attn_heads = jnp.concatenate(head_outputs, axis=1)
    attn_term = jnp.dot(attn_heads, w_out, preferred_element_type=jnp.float32)
    column_groups = model_width // (2 * slice_width)
    attn_blocks = attn_term.reshape(tok_rows, column_groups, 2, slice_width)
    kept = lax.dynamic_index_in_dim(attn_blocks, tc, axis=2, keepdims=False)
    given = lax.dynamic_index_in_dim(attn_blocks, 1 - tc, axis=2, keepdims=False)
    chip_sum = kept + lax.ppermute(given.astype(jnp.bfloat16), "tc", swap).astype(jnp.float32)
    hidden_blocks = hidden.astype(jnp.float32).reshape(tok_rows, column_groups, 2, slice_width)
    chip_axes = ("th", "tl")
    chip_index = th * lax.axis_size("tl") + tl
    chips = column_groups
    shifts = range(1, chips)
    block_sum = lax.dynamic_index_in_dim(chip_sum, chip_index, axis=1, keepdims=False)
    for shift in shifts:
        outgoing = lax.dynamic_index_in_dim(
            chip_sum, (chip_index + shift) % chips, axis=1, keepdims=False
        ).astype(jnp.bfloat16)
        ring = [(src, (src + shift) % chips) for src in range(chips)]
        block_sum = block_sum + lax.ppermute(outgoing, chip_axes, ring).astype(jnp.float32)
    shared = block_sum.astype(jnp.bfloat16)
    gathered = jnp.stack(
        [block_sum]
        + [
            lax.ppermute(shared, chip_axes, [(src, (src + shift) % chips) for src in range(chips)]).astype(
                jnp.float32
            )
            for shift in shifts
        ]
    )
    order = (chip_index - jnp.arange(chips, dtype=jnp.int32)) % chips
    full_sum = jnp.take(gathered, order, axis=0).transpose(1, 0, 2)
    residual = lax.dynamic_index_in_dim(hidden_blocks, tc, axis=2, keepdims=False) + full_sum
    own_squares = jnp.sum(residual * residual, axis=(1, 2))
    all_squares = own_squares + lax.ppermute(own_squares, "tc", swap)
    gain_here = lax.dynamic_index_in_dim(
        moe_gain.reshape(column_groups, 2, slice_width), tc, axis=1, keepdims=False
    )
    normed_half = (
        residual * lax.rsqrt(all_squares / model_width + norm_eps)[:, None, None] * gain_here
    ).astype(jnp.bfloat16).reshape(tok_rows, column_groups * slice_width)
    residual_share = lax.dynamic_index_in_dim(
        residual, th * lax.axis_size("tl") + tl, axis=1, keepdims=False
    )
    experts_here = EXPERTS // req_count
    units_dev = w_down.shape[1]
    tok_ids = jnp.arange(tok_rows, dtype=jnp.int32)
    route_hot = (routes[:, :, None] == jnp.arange(EXPERTS, dtype=jnp.int32)).astype(jnp.float32)
    per_token = jnp.sum(route_hot, axis=1)
    weight_of = jnp.sum(route_weights[:, :, None] * route_hot, axis=1)
    earlier = (tok_ids[:, None] > tok_ids[None, :]).astype(jnp.bfloat16)
    slot_of = jnp.dot(earlier, per_token.astype(jnp.bfloat16), preferred_element_type=jnp.float32)
    capacity = CAP
    cap_ids = jnp.arange(capacity, dtype=jnp.float32)
    picked_here = lax.dynamic_index_in_dim(
        per_token.reshape(tok_rows, req_count, experts_here), th, axis=2, keepdims=False
    ).T
    slot_here = lax.dynamic_index_in_dim(
        slot_of.reshape(tok_rows, req_count, experts_here), th, axis=2, keepdims=False
    ).T
    select = jnp.where(
        (picked_here[:, None, :] > 0.5) & (slot_here[:, None, :] == cap_ids[None, :, None]), 1.0, 0.0
    ).astype(jnp.bfloat16)
    send_rows = jnp.einsum(
        "ict,tw->icw", select, normed_half, preferred_element_type=jnp.float32
    ).astype(jnp.bfloat16)
    req_index = lax.axis_index("req")
    arrivals = [lax.dynamic_index_in_dim(send_rows, req_index, axis=0, keepdims=False)]
    for shift in range(1, req_count):
        outgoing = lax.dynamic_index_in_dim(
            send_rows, (req_index + shift) % req_count, axis=0, keepdims=False
        )
        ring = [(src, (src + shift) % req_count) for src in range(req_count)]
        arrivals.append(lax.ppermute(outgoing, "req", ring))
    source_order = (req_index - jnp.arange(req_count, dtype=jnp.int32)) % req_count
    received = jnp.take(jnp.stack(arrivals), source_order, axis=0)
    partner_rows = lax.ppermute(received, "tc", [(0, 1), (1, 0)])
    weight_blocks = w_gate_up[0].reshape(column_groups, 2, slice_width, 2, units_dev)
    own_weights = lax.dynamic_index_in_dim(weight_blocks, tc, axis=1, keepdims=False).reshape(
        model_width // 2, 2, units_dev
    )
    partner_weights = lax.dynamic_index_in_dim(
        weight_blocks, 1 - tc, axis=1, keepdims=False
    ).reshape(model_width // 2, 2, units_dev)
    gate_up = jnp.einsum(
        "scw,wgu->scgu", received, own_weights, preferred_element_type=jnp.float32
    ) + jnp.einsum(
        "scw,wgu->scgu", partner_rows, partner_weights, preferred_element_type=jnp.float32
    )
    activated = (jax.nn.silu(gate_up[..., 0, :]) * gate_up[..., 1, :]).astype(jnp.bfloat16)
    down = (
        w_down[0]
        .reshape(units_dev, 2, 2, 2, slice_width)
        .transpose(0, 3, 2, 1, 4)
        .reshape(units_dev, model_width)
    )
    partial = jnp.einsum(
        "scu,uw->scw", activated, down, preferred_element_type=jnp.float32
    ).astype(jnp.bfloat16)
    swap = [(0, 1), (1, 0)]
    half = model_width // 2
    kept = lax.dynamic_slice_in_dim(partial, tc * half, half, 2)
    given = lax.dynamic_slice_in_dim(partial, (1 - tc) * half, half, 2)
    pair_sum = kept.astype(jnp.float32) + lax.ppermute(given, "tc", swap).astype(jnp.float32)
    quarter = half // 2
    kept = lax.dynamic_slice_in_dim(pair_sum, tl * quarter, quarter, 2)
    given = lax.dynamic_slice_in_dim(pair_sum, (1 - tl) * quarter, quarter, 2).astype(jnp.bfloat16)
    quad_sum = (kept + lax.ppermute(given, "tl", swap).astype(jnp.float32)).astype(jnp.bfloat16)
    back = (
        quad_sum.reshape(req_count, capacity, 2, slice_width)
        .transpose(0, 2, 1, 3)
        .reshape(req_count * 2, capacity, slice_width)
    )
    returned = lax.all_to_all(back, ("req", "th"), 0, 0, tiled=True)
    combine = weight_of[:, :, None] * (slot_of[:, :, None] == cap_ids[None, None, :])
    mixture = jnp.dot(
        combine.reshape(tok_rows, EXPERTS * capacity),
        returned.reshape(EXPERTS * capacity, slice_width).astype(jnp.float32),
        precision=lax.Precision.HIGHEST,
        preferred_element_type=jnp.float32,
    )
    output = (residual_share + mixture).astype(jnp.bfloat16)
    picked_rows = (jnp.arange(req_local, dtype=jnp.int32)[:, None] * draft_len + accepted).reshape(
        -1
    )
    accepted_kv = jnp.stack(
        [keys_new.reshape(tok_rows, feat_dev)[picked_rows], values_new[picked_rows]]
    )
    return (output, accepted_kv)


def solution(mesh):
    req_count = mesh.shape["req"]
    devices = mesh.devices.reshape(req_count, 2, 2, mesh.shape["tp"] // 4)
    split_mesh = Mesh(devices, ("req",) + TP)
    return jax.shard_map(
        local,
        mesh=split_mesh,
        in_specs=(
            P("req", None),
            P(None, "req", None, TP),
            P("req", None),
            P("req"),
            P("req", None),
            P("req", None),
            P(),
            P(None, None, TP),
            P(None, TP),
            P(TP, None),
            P(),
            P("req", None),
            P("req", None),
            P("req", None, None, TP),
            P("req", TP, None),
        ),
        out_specs=(P("req", TP), P(None, "req", TP)),
        check_vma=False,
    )
```

```python
import jax
import jax.numpy as jnp
from jax import lax
from jax.sharding import Mesh, PartitionSpec as P

HD = 128
FFE = 1024
EXPERTS = 64
CAP = 40
TP = ("th", "tl", "tc")


norm_eps = 1e-05
rope_base = 10000.0
masked_score = -1e30


def rms_scale(values, gain):
    return values * lax.rsqrt(jnp.mean(values * values, axis=-1, keepdims=True) + norm_eps) * gain


def tree_masks(parents):
    slot_count = parents.shape[-1]
    slot_ids = jnp.arange(slot_count, dtype=jnp.int32)
    parent_hot = (parents[..., :, None] == slot_ids).astype(jnp.float32)
    ancestry = jnp.minimum(jnp.eye(slot_count, dtype=jnp.float32) + parent_hot, 1.0)
    for squaring in range(slot_count.bit_length()):
        hops = ancestry.astype(jnp.bfloat16)
        ancestry = jnp.minimum(
            jnp.einsum("rij,rjk->rik", hops, hops, preferred_element_type=jnp.float32), 1.0
        )
    depths = jnp.sum(ancestry, axis=-1).astype(jnp.int32) - 1
    return (ancestry, depths)


def rotate(values, positions):
    head_dim = values.shape[-1]
    half_dim = head_dim // 2
    frequency = rope_base ** (-jnp.arange(half_dim, dtype=jnp.float32) * 2.0 / head_dim)
    angles = positions.astype(jnp.float32)[:, None] * frequency[None, :]
    cosine = jnp.cos(angles)[:, None, :]
    sine_part = jnp.sin(angles)[:, None, :]
    first_half = values[..., :half_dim]
    second = values[..., half_dim:]
    return jnp.concatenate(
        [first_half * cosine - second * sine_part, second * cosine + first_half * sine_part],
        axis=-1,
    )


def local(
    hidden,
    kv_cache,
    page_table,
    cache_lens,
    parents,
    accepted,
    attn_gain,
    w_qkv,
    qk_gain,
    w_out,
    moe_gain,
    routes,
    route_weights,
    w_gate_up,
    w_down,
):
    tok_rows, model_width = hidden.shape
    th = lax.axis_index("th")
    tl = lax.axis_index("tl")
    tc = lax.axis_index("tc")
    tp_count = lax.axis_size(TP)
    req_count = lax.axis_size("req")
    slice_width = model_width // tp_count
    slice_start = ((th * lax.axis_size("tl") + tl) * lax.axis_size("tc") + tc) * slice_width
    req_local, draft_len = parents.shape
    feat_dev = w_qkv.shape[2]
    local_heads = feat_dev // HD
    ancestry, depths = tree_masks(parents)
    positions = (cache_lens[:, None] + depths).reshape(-1)
    normed_in = rms_scale(hidden.astype(jnp.float32), attn_gain).astype(jnp.bfloat16)
    projected = jnp.einsum(
        "tw,wgf->tgf", normed_in, w_qkv, preferred_element_type=jnp.float32
    )
    query_raw = projected[:, 0]
    key_raw = projected[:, 1]
    values_new = projected[:, 2].astype(jnp.bfloat16)
    swap = [(0, 1), (1, 0)]
    squares = jnp.stack(
        [jnp.sum(query_raw * query_raw, axis=-1), jnp.sum(key_raw * key_raw, axis=-1)]
    )
    tp_ring = [[(src, (src + shift) % tp_count) for src in range(tp_count)] for shift in range(1, tp_count)]
    squares = squares + sum(lax.ppermute(squares, TP, ring) for ring in tp_ring)
    query_normed = query_raw * lax.rsqrt(squares[0][:, None] / model_width + norm_eps) * qk_gain[0]
    key_normed = key_raw * lax.rsqrt(squares[1][:, None] / model_width + norm_eps) * qk_gain[1]
    query_rot = rotate(query_normed.reshape(tok_rows, local_heads, HD), positions).astype(
        jnp.bfloat16
    )
    keys_new = rotate(key_normed.reshape(tok_rows, local_heads, HD), positions).astype(jnp.bfloat16)
    local_pages, page_len = kv_cache.shape[1], kv_cache.shape[2]
    all_keys = kv_cache[0].reshape(local_pages * page_len, feat_dev)
    all_values = kv_cache[1].reshape(local_pages * page_len, feat_dev)
    page_ids = jnp.arange(local_pages, dtype=jnp.int32)
    page_match = (page_table[:, :, None] == page_ids[None, None, :]).astype(jnp.int32)
    page_owned = jnp.sum(page_match, axis=1)
    page_start = jnp.sum(
        page_match * (jnp.arange(page_table.shape[1], dtype=jnp.int32) * page_len)[None, :, None],
        axis=1,
    )
    key_pos = (page_start[:, :, None] + jnp.arange(page_len, dtype=jnp.int32)[None, None, :]).reshape(
        req_local, local_pages * page_len
    )
    live_keys = (jnp.repeat(page_owned, page_len, axis=1) > 0) & (key_pos < cache_lens[:, None])
    score_scale = HD ** (-0.5)
    queries = query_rot.reshape(req_local, draft_len, local_heads, HD)
    own_keys = keys_new.reshape(req_local, draft_len, local_heads, HD)
    own_values = values_new.reshape(req_local, draft_len, local_heads, HD)
    head_keys = all_keys.reshape(local_pages * page_len, local_heads, HD)
    head_values = all_values.reshape(local_pages * page_len, local_heads, HD)
    cache_scores = (
        jnp.einsum("rjhd,chd->rhjc", queries, head_keys, preferred_element_type=jnp.float32)
        * score_scale
    )
    cache_scores = jnp.where(live_keys[:, None, None, :], cache_scores, masked_score)
    draft_scores = (
        jnp.einsum("rjhd,rihd->rhji", queries, own_keys, preferred_element_type=jnp.float32)
        * score_scale
    )
    draft_scores = jnp.where(ancestry[:, None] > 0.5, draft_scores, masked_score)
    row_max = jnp.maximum(
        jnp.max(cache_scores, axis=-1, keepdims=True),
        jnp.max(draft_scores, axis=-1, keepdims=True),
    )
    cache_weights = jnp.exp(cache_scores - row_max)
    draft_weights = jnp.exp(draft_scores - row_max)
    total = jnp.sum(cache_weights, axis=-1, keepdims=True) + jnp.sum(
        draft_weights, axis=-1, keepdims=True
    )
    cache_probs = (cache_weights / total).astype(jnp.bfloat16)
    draft_probs = (draft_weights / total).astype(jnp.bfloat16)
    attn_heads = (
        jnp.einsum("rhjc,chd->rjhd", cache_probs, head_values, preferred_element_type=jnp.float32)
        + jnp.einsum("rhji,rihd->rjhd", draft_probs, own_values, preferred_element_type=jnp.float32)
    ).astype(jnp.bfloat16).reshape(tok_rows, feat_dev)
    attn_term = jnp.dot(attn_heads, w_out, preferred_element_type=jnp.float32)
    column_groups = model_width // (2 * slice_width)
    attn_blocks = attn_term.reshape(tok_rows, column_groups, 2, slice_width)
    kept = lax.dynamic_index_in_dim(attn_blocks, tc, axis=2, keepdims=False)
    given = lax.dynamic_index_in_dim(attn_blocks, 1 - tc, axis=2, keepdims=False)
    chip_sum = kept + lax.ppermute(given.astype(jnp.bfloat16), "tc", swap).astype(jnp.float32)
    hidden_blocks = hidden.astype(jnp.float32).reshape(tok_rows, column_groups, 2, slice_width)
    chip_axes = ("th", "tl")
    chip_index = th * lax.axis_size("tl") + tl
    chips = column_groups
    shifts = range(1, chips)
    block_sum = lax.dynamic_index_in_dim(chip_sum, chip_index, axis=1, keepdims=False)
    for shift in shifts:
        outgoing = lax.dynamic_index_in_dim(
            chip_sum, (chip_index + shift) % chips, axis=1, keepdims=False
        ).astype(jnp.bfloat16)
        ring = [(src, (src + shift) % chips) for src in range(chips)]
        block_sum = block_sum + lax.ppermute(outgoing, chip_axes, ring).astype(jnp.float32)
    shared = block_sum.astype(jnp.bfloat16)
    gathered = jnp.stack(
        [block_sum]
        + [
            lax.ppermute(shared, chip_axes, [(src, (src + shift) % chips) for src in range(chips)]).astype(
                jnp.float32
            )
            for shift in shifts
        ]
    )
    order = (chip_index - jnp.arange(chips, dtype=jnp.int32)) % chips
    full_sum = jnp.take(gathered, order, axis=0).transpose(1, 0, 2)
    residual = lax.dynamic_index_in_dim(hidden_blocks, tc, axis=2, keepdims=False) + full_sum
    own_squares = jnp.sum(residual * residual, axis=(1, 2))
    all_squares = own_squares + lax.ppermute(own_squares, "tc", swap)
    gain_here = lax.dynamic_index_in_dim(
        moe_gain.reshape(column_groups, 2, slice_width), tc, axis=1, keepdims=False
    )
    normed_half = (
        residual * lax.rsqrt(all_squares / model_width + norm_eps)[:, None, None] * gain_here
    ).astype(jnp.bfloat16).reshape(tok_rows, column_groups * slice_width)
    residual_share = lax.dynamic_index_in_dim(
        residual, th * lax.axis_size("tl") + tl, axis=1, keepdims=False
    )
    experts_here = EXPERTS // req_count
    units_dev = w_down.shape[1]
    tok_ids = jnp.arange(tok_rows, dtype=jnp.int32)
    route_hot = (routes[:, :, None] == jnp.arange(EXPERTS, dtype=jnp.int32)).astype(jnp.float32)
    per_token = jnp.sum(route_hot, axis=1)
    weight_of = jnp.sum(route_weights[:, :, None] * route_hot, axis=1)
    earlier = (tok_ids[:, None] > tok_ids[None, :]).astype(jnp.bfloat16)
    slot_of = jnp.dot(earlier, per_token.astype(jnp.bfloat16), preferred_element_type=jnp.float32)
    capacity = CAP
    cap_ids = jnp.arange(capacity, dtype=jnp.float32)
    picked_here = lax.dynamic_index_in_dim(
        per_token.reshape(tok_rows, req_count, experts_here), th, axis=2, keepdims=False
    ).T
    slot_here = lax.dynamic_index_in_dim(
        slot_of.reshape(tok_rows, req_count, experts_here), th, axis=2, keepdims=False
    ).T
    select = jnp.where(
        (picked_here[:, None, :] > 0.5) & (slot_here[:, None, :] == cap_ids[None, :, None]), 1.0, 0.0
    ).astype(jnp.bfloat16)
    send_rows = jnp.einsum(
        "ict,tw->icw", select, normed_half, preferred_element_type=jnp.float32
    ).astype(jnp.bfloat16)
    received = lax.all_to_all(send_rows, "req", 0, 0, tiled=True)
    partner_rows = lax.ppermute(received, "tc", [(0, 1), (1, 0)])
    weight_blocks = w_gate_up[0].reshape(column_groups, 2, slice_width, 2, units_dev)
    own_weights = lax.dynamic_index_in_dim(weight_blocks, tc, axis=1, keepdims=False).reshape(
        model_width // 2, 2, units_dev
    )
    partner_weights = lax.dynamic_index_in_dim(
        weight_blocks, 1 - tc, axis=1, keepdims=False
    ).reshape(model_width // 2, 2, units_dev)
    gate_up = jnp.einsum(
        "scw,wgu->scgu", received, own_weights, preferred_element_type=jnp.float32
    ) + jnp.einsum(
        "scw,wgu->scgu", partner_rows, partner_weights, preferred_element_type=jnp.float32
    )
    activated = (jax.nn.silu(gate_up[..., 0, :]) * gate_up[..., 1, :]).astype(jnp.bfloat16)
    down = (
        w_down[0]
        .reshape(units_dev, 2, 2, 2, slice_width)
        .transpose(0, 3, 2, 1, 4)
        .reshape(units_dev, model_width)
    )
    partial = jnp.einsum(
        "scu,uw->scw", activated, down, preferred_element_type=jnp.float32
    ).astype(jnp.bfloat16)
    swap = [(0, 1), (1, 0)]
    half = model_width // 2
    kept = lax.dynamic_slice_in_dim(partial, tc * half, half, 2)
    given = lax.dynamic_slice_in_dim(partial, (1 - tc) * half, half, 2)
    pair_sum = kept.astype(jnp.float32) + lax.ppermute(given, "tc", swap).astype(jnp.float32)
    quarter = half // 2
    kept = lax.dynamic_slice_in_dim(pair_sum, tl * quarter, quarter, 2)
    given = lax.dynamic_slice_in_dim(pair_sum, (1 - tl) * quarter, quarter, 2).astype(jnp.bfloat16)
    quad_sum = (kept + lax.ppermute(given, "tl", swap).astype(jnp.float32)).astype(jnp.bfloat16)
    back = (
        quad_sum.reshape(req_count, capacity, 2, slice_width)
        .transpose(0, 2, 1, 3)
        .reshape(req_count * 2, capacity, slice_width)
    )
    returned = lax.all_to_all(back, ("req", "th"), 0, 0, tiled=True)
    combine = weight_of[:, :, None] * (slot_of[:, :, None] == cap_ids[None, None, :])
    mixture = jnp.dot(
        combine.reshape(tok_rows, EXPERTS * capacity),
        returned.reshape(EXPERTS * capacity, slice_width).astype(jnp.float32),
        precision=lax.Precision.HIGHEST,
        preferred_element_type=jnp.float32,
    )
    output = (residual_share + mixture).astype(jnp.bfloat16)
    picked_rows = (jnp.arange(req_local, dtype=jnp.int32)[:, None] * draft_len + accepted).reshape(
        -1
    )
    accepted_kv = jnp.stack(
        [keys_new.reshape(tok_rows, feat_dev)[picked_rows], values_new[picked_rows]]
    )
    return (output, accepted_kv)


def solution(mesh):
    req_count = mesh.shape["req"]
    devices = mesh.devices.reshape(req_count, 2, 2, mesh.shape["tp"] // 4)
    split_mesh = Mesh(devices, ("req",) + TP)
    return jax.shard_map(
        local,
        mesh=split_mesh,
        in_specs=(
            P("req", None),
            P(None, "req", None, TP),
            P("req", None),
            P("req"),
            P("req", None),
            P("req", None),
            P(),
            P(None, None, TP),
            P(None, TP),
            P(TP, None),
            P(),
            P("req", None),
            P("req", None),
            P("req", None, None, TP),
            P("req", TP, None),
        ),
        out_specs=(P("req", TP), P(None, "req", TP)),
        check_vma=False,
    )
```
